256 devices in a mesh: gx: 32 (over z, y), gy: 4 (over x_lo, core), ga: 2 (over x_hi).
Axes of the slice: x: 4 (x_hi: 2, x_lo: 2; x = x_hi * 2 + x_lo), y: 4, z: 8, core: 2. Of those that a mesh axis runs over, the one named last changes fastest.
Arguments:
- velocity: float32 [2, 80, 64, 4096], P(None, None, ('gy', 'ga'), 'gx'), may hold values from -4 to 4
- tracers: float32 [2, 80, 64, 4096], P(None, None, ('gy', 'ga'), 'gx'), may hold values from -6 to 6
- mixing: float32 [80, 64, 4096], P(None, ('gy', 'ga'), 'gx'), may hold values from 0.05 to 400
- thickness: float32 [80], replicated, may hold values from 0.5 to 4
- coriolis: float32 [64], P(('gy', 'ga')), may hold values from -1.5 to 1.5
- land: int32 [64, 4096], P(('gy', 'ga'), 'gx'), may hold values 0 or 1
- bottom: int32 [64, 4096], P(('gy', 'ga'), 'gx'), may hold values from 70 to 80
- surface: float32 [64, 4096], P(('gy', 'ga'), 'gx'), may hold values from -4 to 4
- barotropic: float32 [2, 64, 4096], P(None, ('gy', 'ga'), 'gx'), may hold values from -3 to 3
Outputs:
- new_velocity: float32 [2, 80, 64, 4096], P(None, None, ('gy', 'ga'), 'gx')
- new_tracers: float32 [2, 80, 64, 4096], P(None, None, ('gy', 'ga'), 'gx')
- new_surface: float32 [64, 4096], P(('gy', 'ga'), 'gx')
- new_barotropic: float32 [2, 64, 4096], P(None, ('gy', 'ga'), 'gx')
The draws below stay inside these ranges and needn't reach their ends.
All inputs are finite; a program needn't handle non-finite values. No bound on the sum of `land` on one device may be relied on, other than what follows from the above.
Results may differ from the reference program's by a relative error of at most 0.0003.
Values sent between devices are 32-bit elements; how exact they have to be, the bound alone decides.
No kernel may reach another device: no remote copies, remote signals or barrier semaphores. Data moves between devices by JAX's collectives and lax.ppermute only.
A program may use at most 64 MiB of HBM per device.

```python
import math
import jax
import jax.numpy as jnp
from jax import lax

NZ = 80
NSUB = 30
NX = 4096
NY = 64
N_GX = 32


def draw_mixing(key, part):
    base_key, rough_key = jax.random.split(jax.random.fold_in(key, 11))
    lowest = 0.1
    base = jnp.exp(jax.random.uniform(base_key, (NY, NX), jnp.float32, math.log(lowest), math.log(200.0)))
    rough = jnp.exp(jax.random.uniform(rough_key, (NZ, NY, NX), jnp.float32, math.log(0.5), math.log(2.0)))
    return base[None] * rough


def draw_surface(key, part):
    noise_key = jax.random.fold_in(jax.random.fold_in(key, 23), 0)
    return 0.5 * jax.random.truncated_normal(noise_key, -8.0, 8.0, (NY, NX), jnp.float32)


def set_ends(entries, rng, smallest, largest):
    spot = [jax.random.randint(jax.random.fold_in(rng, axis), (), 0, length) for axis, length in enumerate(entries.shape)]
    widest = entries.shape.index(max(entries.shape))
    next_to = spot[:widest] + [(spot[widest] + 1) % entries.shape[widest]] + spot[widest + 1:]
    return entries.at[tuple(spot)].set(smallest).at[tuple(next_to)].set(largest)


def level_of(rng, shape, cuts, smallest, top_value):
    gain, own = 1.0, jax.random.fold_in(rng, 6)
    for axis_at, blocks in cuts:
        steps = jnp.exp(jax.random.uniform(jax.random.fold_in(own, axis_at), (blocks,), jnp.float32, smallest / len(cuts), top_value / len(cuts)))
        gain = gain * jnp.repeat(steps, shape[axis_at] // blocks).reshape([-1 if axis == axis_at else 1 for axis in range(len(shape))])
    return gain


def noise(rng, dims, spread, limit, shards=(), kind=jnp.bfloat16):
    array = jax.random.normal(rng, dims, jnp.float32) * spread
    if len(shards) > 0:
        array = level_of(rng, dims, shards, -0.22, 0.18) * array
    return jnp.clip(array, min=-limit, max=limit).astype(kind)


def setup_inputs(seed: int = 0) -> dict:
    splits = jax.random.split(jax.random.key(seed), 10)
    velocity = noise(splits[0], (2, NZ, NY, NX), 0.5, 4.0, ((2, 8), (3, 32)), jnp.float32)
    tracers = noise(splits[1], (2, NZ, NY, NX), 1.0, 6.0, ((2, 8), (3, 32)), jnp.float32)
    mixing = draw_mixing(jax.random.fold_in(splits[9], 71), 0)
    thickness = jnp.clip(jnp.exp(jax.random.uniform(splits[3], (NZ,), jnp.float32, math.log(0.5), math.log(4.0))), 0.5, 4.0)
    coriolis = jnp.clip(jax.random.uniform(splits[4], (NY,), jnp.float32, -1.5, 1.5) * level_of(splits[4], (NY,), ((0, 8),), -0.4, 0.0), -1.5, 1.5)
    land = set_ends((jax.random.randint(splits[5], (NY, NX), 0, 50) < 49).astype(jnp.int32), jax.random.fold_in(splits[5], 1), 0, 1)
    bottom = set_ends(jax.random.randint(splits[6], (NY, NX), NZ - NZ // 8, NZ + 1), jax.random.fold_in(splits[6], 1), NZ - NZ // 8, NZ).astype(jnp.int32)
    surface = draw_surface(jax.random.fold_in(splits[9], 71), 0)
    barotropic = noise(splits[8], (2, NY, NX), 0.3, 3.0, ((1, 8), (2, 32)), jnp.float32)
    return dict(velocity=velocity, tracers=tracers, mixing=mixing, thickness=thickness, coriolis=coriolis, land=land, bottom=bottom, surface=surface, barotropic=barotropic)


step_main = 0.1
visc_four = 0.02
diff_four = 0.02
press_scale = 0.02
step_baro = 0.1
grav_baro = 25.0
expand_temp = 0.2
contract_salt = 0.1


def laplace(quantity, wet_mask):
    centre = quantity[..., 1:-1, 1:-1]
    beside_all = quantity[..., 1:-1, 2:] + quantity[..., 1:-1, :-2] + quantity[..., 2:, 1:-1] + quantity[..., :-2, 1:-1]
    return (beside_all - 4.0 * centre) * wet_mask[..., 1:-1, 1:-1]


def diff_x(quantity):
    return 0.5 * (quantity[..., 2:-2, 3:-1] - quantity[..., 2:-2, 1:-3])


def diff_y(quantity):
    return 0.5 * (quantity[..., 3:-1, 2:-2] - quantity[..., 1:-3, 2:-2])


def tendency(padded, pressure, coriolis):
    east_vel = padded[0]
    north_vel = padded[1]
    wet_mask = padded[4]
    inner_wet = wet_mask[..., 2:-2, 2:-2]
    rotate = coriolis[:, None]
    changes = []
    for component in range(4):
        quantity = padded[component]
        advect = diff_x(east_vel * quantity) + diff_y(north_vel * quantity)
        smooth = laplace(laplace(quantity, wet_mask), wet_mask[..., 1:-1, 1:-1])
        if component == 0:
            change = rotate * north_vel[..., 2:-2, 2:-2] - diff_x(pressure) - visc_four * smooth
        elif component == 1:
            change = -rotate * east_vel[..., 2:-2, 2:-2] - diff_y(pressure) - visc_four * smooth
        else:
            change = -diff_four * smooth
        changes.append((change - advect) * inner_wet)
    return jnp.stack(changes)


def vertical_solve(provisional, mixing, wet_mask, thickness):
    levels = thickness.shape[0]
    tail_ones = (1,) * (mixing.ndim - 1)
    depth_col = thickness.reshape((levels,) + tail_ones)
    middle = (0.5 * (thickness[:-1] + thickness[1:])).reshape((levels - 1,) + tail_ones)
    coupling = mixing[:-1] * wet_mask[:-1] * wet_mask[1:] / middle
    zeros_row = jnp.zeros((1,) + mixing.shape[1:], jnp.float32)
    below_link = jnp.concatenate([coupling, zeros_row], axis=0)
    upper_link = jnp.concatenate([zeros_row, coupling], axis=0)
    diagonal = depth_col + upper_link + below_link
    source = depth_col[:, None] * provisional

    def forward(sweep, inputs):
        ratio_prev, value_prev = sweep
        upper_now, diag_now, below_now, source_now = inputs
        divisor = diag_now - upper_now * ratio_prev
        sweep_ratio = below_now / divisor
        sweep_value = (source_now + upper_now[None] * value_prev) / divisor[None]
        return (sweep_ratio, sweep_value), (sweep_ratio, sweep_value)

    start_sweep = (jnp.zeros(mixing.shape[1:], jnp.float32), jnp.zeros(provisional.shape[1:], jnp.float32))
    unused, (ratios, values) = lax.scan(forward, start_sweep, (upper_link, diagonal, below_link, source))

    def backward(following, inputs):
        sweep_ratio, sweep_value = inputs
        result = sweep_value + sweep_ratio[None] * following
        return result, result

    unused_last, solved = lax.scan(backward, jnp.zeros(provisional.shape[1:], jnp.float32), (ratios, values), reverse=True)
    return solved


def zero_diff(quantity, along):
    extent = quantity.shape[along]
    ahead_part = lax.slice_in_dim(quantity, 1, extent, axis=along)
    behind = lax.slice_in_dim(quantity, 0, extent - 1, axis=along)
    zeros_row = jnp.zeros_like(lax.slice_in_dim(quantity, 0, 1, axis=along))
    return 0.5 * (jnp.concatenate([ahead_part, zeros_row], axis=along) - jnp.concatenate([zeros_row, behind], axis=along))


def roll_east(quantity):
    return 0.5 * (jnp.roll(quantity, -1, axis=-1) - jnp.roll(quantity, 1, axis=-1))


def north_zero(quantity):
    return zero_diff(quantity, quantity.ndim - 2)


def baro_step(baro_state, statics, east_diff, north_diff):
    height = baro_state[0]
    east_vel = baro_state[1]
    north_vel = baro_state[2]
    depth_ratio = statics[0]
    sea_mask = statics[1]
    rotate = statics[2]
    push_east = statics[3]
    push_north = statics[4]
    new_height = (height - step_baro * (east_diff(depth_ratio * east_vel) + north_diff(depth_ratio * north_vel))) * sea_mask
    new_east = (east_vel + step_baro * (push_east + rotate * north_vel - grav_baro * east_diff(new_height))) * sea_mask
    new_north = (north_vel + step_baro * (push_north - rotate * east_vel - grav_baro * north_diff(new_height))) * sea_mask
    return jnp.stack([new_height, new_east, new_north])


def pad_field(quantity, halo_width):
    wrapped = jnp.concatenate([quantity[..., -halo_width:], quantity, quantity[..., :halo_width]], axis=-1)
    zeros_rows = jnp.zeros(wrapped.shape[:-2] + (halo_width, wrapped.shape[-1]), jnp.float32)
    return jnp.concatenate([zeros_rows, wrapped, zeros_rows], axis=-2)


def reference(velocity, tracers, mixing, thickness, coriolis, land, bottom, surface, barotropic):
    levels = thickness.shape[0]
    land_f = land.astype(jnp.float32)

    def level_step(loop_carry, level_index):
        overlying, forcing, depth_sum = loop_carry
        wet_level = land_f * (level_index < bottom).astype(jnp.float32)
        velocity_level = lax.dynamic_index_in_dim(velocity, level_index, 1, keepdims=False) * wet_level[None]
        tracer_level = lax.dynamic_index_in_dim(tracers, level_index, 1, keepdims=False) * wet_level[None]
        stacked = jnp.concatenate([velocity_level, tracer_level, wet_level[None]], axis=0)
        padded = pad_field(stacked, 2)
        layer_dz = thickness[level_index]
        weight = (contract_salt * padded[3] - expand_temp * padded[2]) * padded[4] * layer_dz
        pressure = press_scale * (overlying + 0.5 * weight)
        growth = tendency(padded, pressure, coriolis)
        provisional = stacked[:4] + step_main * growth
        return (overlying + weight, forcing + layer_dz * growth[:2], depth_sum + layer_dz * wet_level), provisional

    start_carry = (jnp.zeros((land.shape[0] + 4, land.shape[1] + 4), jnp.float32),
                   jnp.zeros((2,) + land.shape, jnp.float32), jnp.zeros(land.shape, jnp.float32))
    (unused, forcing, depth_sum), provisional = lax.scan(level_step, start_carry, jnp.arange(levels, dtype=jnp.int32))

    level_ids = jnp.arange(levels, dtype=jnp.int32).reshape((levels, 1, 1))
    wet_full = land_f[None] * (level_ids < bottom[None]).astype(jnp.float32)

    blocks = N_GX
    block_cols = land.shape[1] // blocks

    def block_solve(block_index):
        start = (block_index * block_cols).astype(jnp.int32)
        return vertical_solve(lax.dynamic_slice_in_dim(provisional, start, block_cols, 3),
                              lax.dynamic_slice_in_dim(mixing, start, block_cols, 2),
                              lax.dynamic_slice_in_dim(wet_full, start, block_cols, 2), thickness)

    pieces = lax.map(block_solve, jnp.arange(blocks, dtype=jnp.int32))
    solved = jnp.moveaxis(pieces, 0, -2).reshape(provisional.shape)

    safe_depth = jnp.maximum(depth_sum, 1.0)
    statics = jnp.stack([depth_sum / jnp.sum(thickness), land_f, coriolis[:, None] * jnp.ones_like(land_f),
                         forcing[0] / safe_depth * land_f, forcing[1] / safe_depth * land_f])
    start_state = jnp.concatenate([surface[None], barotropic], axis=0)

    def substep(turn_index, loop_carry):
        baro_state, total_sum = loop_carry
        baro_state = baro_step(baro_state, statics, roll_east, north_zero)
        return baro_state, total_sum + baro_state[1:]

    baro_state, total_sum = lax.fori_loop(0, NSUB, substep, (start_state, jnp.zeros((2,) + land.shape, jnp.float32)))
    average = total_sum / NSUB

    thick_col = thickness.reshape((levels, 1, 1, 1))
    depth_mean = jnp.sum(thick_col * wet_full[:, None] * solved[:, :2], axis=0) / safe_depth
    new_velocity = (jnp.moveaxis(solved[:, :2], 0, 1) - depth_mean[:, None] + average[:, None]) * wet_full[None]
    new_tracers = jnp.moveaxis(solved[:, 2:], 0, 1)
    return new_velocity, new_tracers, baro_state[0], baro_state[1:]
```

```python
import jax
import jax.numpy as jnp
from jax import lax
from jax.sharding import PartitionSpec as P
from jax.experimental import pallas as pl
from jax.experimental.pallas import tpu as pltpu

NSUB = 30


step_main = 0.1
visc_four = 0.02
diff_four = 0.02
press_scale = 0.02
step_baro = 0.1
grav_baro = 25.0
expand_temp = 0.2
contract_salt = 0.1


def padded_2(block, sides, width, periodic):
    for axis, dim in sides:
        count = lax.axis_size(axis)
        forward = [(i, i + 1) for i in range(count - 1)]
        if periodic:
            forward.append((count - 1, 0))
        backward = [(target, source) for source, target in forward]
        low = lax.ppermute(
            lax.slice_in_dim(block, block.shape[dim] - width, None, axis=dim), axis, forward
        )
        high = lax.ppermute(lax.slice_in_dim(block, 0, width, axis=dim), axis, backward)
        block = jnp.concatenate([low, block, high], axis=dim)
    return block


def laplace(quantity, wet_mask):
    centre = quantity[..., 1:-1, 1:-1]
    beside_all = (
        quantity[..., 1:-1, 2:]
        + quantity[..., 1:-1, :-2]
        + quantity[..., 2:, 1:-1]
        + quantity[..., :-2, 1:-1]
    )
    return (beside_all - 4.0 * centre) * wet_mask[..., 1:-1, 1:-1]


def diff_x(quantity):
    return 0.5 * (quantity[..., 2:-2, 3:-1] - quantity[..., 2:-2, 1:-3])


def diff_y(quantity):
    return 0.5 * (quantity[..., 3:-1, 2:-2] - quantity[..., 1:-3, 2:-2])


def tendency(padded, pressure, coriolis):
    east_vel = padded[0]
    north_vel = padded[1]
    wet_mask = padded[4]
    inner_wet = wet_mask[..., 2:-2, 2:-2]
    rotate = coriolis[:, None]
    changes = []
    for component in range(4):
        quantity = padded[component]
        advect = diff_x(east_vel * quantity) + diff_y(north_vel * quantity)
        smooth = laplace(laplace(quantity, wet_mask), wet_mask[..., 1:-1, 1:-1])
        if component == 0:
            change = rotate * north_vel[..., 2:-2, 2:-2] - diff_x(pressure) - visc_four * smooth
        elif component == 1:
            change = -rotate * east_vel[..., 2:-2, 2:-2] - diff_y(pressure) - visc_four * smooth
        else:
            change = -diff_four * smooth
        changes.append((change - advect) * inner_wet)
    return jnp.stack(changes)


def vertical_solve(provisional, mixing, wet_mask, thickness):
    levels = thickness.shape[0]
    tail_ones = (1,) * (mixing.ndim - 1)
    depth_col = thickness.reshape((levels,) + tail_ones)
    middle = (0.5 * (thickness[:-1] + thickness[1:])).reshape((levels - 1,) + tail_ones)
    coupling = mixing[:-1] * wet_mask[:-1] * wet_mask[1:] / middle
    zeros_row = jnp.zeros((1,) + mixing.shape[1:], jnp.float32)
    below_link = jnp.concatenate([coupling, zeros_row], axis=0)
    upper_link = jnp.concatenate([zeros_row, coupling], axis=0)
    diagonal = depth_col + upper_link + below_link
    source = depth_col[:, None] * provisional

    def forward(sweep, inputs):
        ratio_prev, value_prev = sweep
        upper_now, diag_now, below_now, source_now = inputs
        divisor = diag_now - upper_now * ratio_prev
        sweep_ratio = below_now / divisor
        sweep_value = (source_now + upper_now[None] * value_prev) / divisor[None]
        return ((sweep_ratio, sweep_value), (sweep_ratio, sweep_value))

    start_sweep = (
        jnp.zeros(mixing.shape[1:], jnp.float32),
        jnp.zeros(provisional.shape[1:], jnp.float32),
    )
    unused, (ratios, values) = lax.scan(
        forward, start_sweep, (upper_link, diagonal, below_link, source)
    )

    def backward(following, inputs):
        sweep_ratio, sweep_value = inputs
        result = sweep_value + sweep_ratio[None] * following
        return (result, result)

    unused_last, solved = lax.scan(
        backward, jnp.zeros(provisional.shape[1:], jnp.float32), (ratios, values), reverse=True
    )
    return solved


def zero_diff(quantity, along):
    extent = quantity.shape[along]
    ahead_part = lax.slice_in_dim(quantity, 1, extent, axis=along)
    behind = lax.slice_in_dim(quantity, 0, extent - 1, axis=along)
    zeros_row = jnp.zeros_like(lax.slice_in_dim(quantity, 0, 1, axis=along))
    return 0.5 * (
        jnp.concatenate([ahead_part, zeros_row], axis=along)
        - jnp.concatenate([zeros_row, behind], axis=along)
    )


def east_zero(quantity):
    return zero_diff(quantity, quantity.ndim - 1)


def north_zero(quantity):
    return zero_diff(quantity, quantity.ndim - 2)


def baro_step(baro_state, statics, east_diff, north_diff):
    height = baro_state[0]
    east_vel = baro_state[1]
    north_vel = baro_state[2]
    depth_ratio = statics[0]
    sea_mask = statics[1]
    rotate = statics[2]
    push_east = statics[3]
    push_north = statics[4]
    new_height = (
        height
        - step_baro * (east_diff(depth_ratio * east_vel) + north_diff(depth_ratio * north_vel))
    ) * sea_mask
    new_east = (
        east_vel + step_baro * (push_east + rotate * north_vel - grav_baro * east_diff(new_height))
    ) * sea_mask
    new_north = (
        north_vel
        + step_baro * (push_north - rotate * east_vel - grav_baro * north_diff(new_height))
    ) * sea_mask
    return jnp.stack([new_height, new_east, new_north])


def zonal_rims(stacked):
    return padded_2(stacked, (("gx", 3),), 2, True)


def merid_rims(stacked):
    return padded_2(stacked, ((("gy", "ga"), 2),), 2, False)


def baro_zonal(operand, halo_width):
    return padded_2(operand, (("gx", 2),), halo_width, True)


def baro_merid_all(operand, halo_width):
    return padded_2(operand, ((("gy", "ga"), 1),), halo_width, False)


def shards(velocity, tracers, mixing, thickness, coriolis, land, bottom, surface, barotropic):
    levels = thickness.shape[0]
    land_f = land.astype(jnp.float32)
    level_ids = lax.broadcasted_iota(jnp.int32, (levels,) + land.shape, 0)
    wet_mask = land_f[None] * (level_ids < bottom[None]).astype(jnp.float32)
    stacked = jnp.concatenate(
        [velocity * wet_mask[None], tracers * wet_mask[None], wet_mask[None]], axis=0
    )
    padded = merid_rims(zonal_rims(stacked))
    depth_col = thickness.reshape((levels, 1, 1))
    weight = (contract_salt * padded[3] - expand_temp * padded[2]) * padded[4] * depth_col
    pressure = press_scale * (jnp.cumsum(weight, axis=0) - weight + 0.5 * weight)
    growth = tendency(padded, pressure, coriolis)
    provisional = stacked[:4] + step_main * growth
    forcing = jnp.sum(depth_col * growth[:2], axis=1)
    depth_sum = jnp.sum(depth_col * wet_mask, axis=0)
    safe_depth = jnp.maximum(depth_sum, 1.0)
    dr = depth_sum / jnp.sum(thickness)
    push_u = forcing[0] / safe_depth * land_f
    push_v = forcing[1] / safe_depth * land_f
    rotate = coriolis[:, None] * jnp.ones_like(land_f)
    fields = jnp.stack([dr, land_f, rotate, push_u, push_v, surface, barotropic[0], barotropic[1]])
    whole = gather_baro(fields)
    baro_out = baro_run(whole)
    rows = land.shape[0]
    cols = land.shape[1]
    merid = lax.axis_index(("gy", "ga"))
    mine = lax.dynamic_slice_in_dim(baro_out, merid * rows, rows, axis=1)[:, :, BARO_HALO:BARO_HALO + cols]
    average = mine[3:] / NSUB
    solved = solve_columns(provisional, mixing, wet_mask, thickness)
    thick_col = thickness.reshape((levels, 1, 1))
    depth_mean = jnp.sum(thick_col[None] * wet_mask[None] * solved[:2], axis=1) / safe_depth
    new_velocity = (solved[:2] - depth_mean[:, None] + average[:, None]) * wet_mask[None]
    new_tracers = solved[2:]
    return (new_velocity, new_tracers, mine[0], mine[1:3])


BARO_HALO = 64


def gather_baro(fields):
    count = lax.axis_size("gx")
    forward = [(i, (i + 1) % count) for i in range(count)]
    backward = [(target, source) for source, target in forward]
    low = lax.ppermute(fields[..., -BARO_HALO:], "gx", forward)
    high = lax.ppermute(fields[..., :BARO_HALO], "gx", backward)
    wide = jnp.concatenate([low, fields, high], axis=-1)
    return lax.all_gather(wide, ("gy", "ga"), axis=1, tiled=True)


def baro_kernel(f_ref, o_ref):
    rows = f_ref.shape[1]
    cols = f_ref.shape[2]
    depth_ratio = f_ref[0]
    sea_mask = f_ref[1]
    rotate = f_ref[2]
    push_east = f_ref[3]
    push_north = f_ref[4]
    row = lax.broadcasted_iota(jnp.int32, (rows, cols), 0)
    not_last = row < rows - 1
    not_first = row > 0

    def east_diff(q):
        return 0.5 * (pltpu.roll(q, cols - 1, 1) - pltpu.roll(q, 1, 1))

    def north_diff(q):
        ahead = jnp.where(not_last, pltpu.roll(q, rows - 1, 0), 0.0)
        behind = jnp.where(not_first, pltpu.roll(q, 1, 0), 0.0)
        return 0.5 * (ahead - behind)

    def body(turn, carry):
        height, east_vel, north_vel, sum_east, sum_north = carry
        height = (
            height
            - step_baro * (east_diff(depth_ratio * east_vel) + north_diff(depth_ratio * north_vel))
        ) * sea_mask
        new_east = (
            east_vel + step_baro * (push_east + rotate * north_vel - grav_baro * east_diff(height))
        ) * sea_mask
        new_north = (
            north_vel
            + step_baro * (push_north - rotate * east_vel - grav_baro * north_diff(height))
        ) * sea_mask
        return (height, new_east, new_north, sum_east + new_east, sum_north + new_north)

    zeros = jnp.zeros((rows, cols), jnp.float32)
    carry = (f_ref[5], f_ref[6], f_ref[7], zeros, zeros)
    carry = lax.fori_loop(0, NSUB, body, carry)
    for index in range(5):
        o_ref[index] = carry[index]


def baro_run(whole):
    return pl.pallas_call(
        baro_kernel,
        out_shape=jax.ShapeDtypeStruct((5,) + whole.shape[1:], jnp.float32),
        in_specs=[pl.BlockSpec(memory_space=pltpu.VMEM)],
        out_specs=pl.BlockSpec(memory_space=pltpu.VMEM),
    )(whole)


def solve_kernel(th_ref, prov_ref, mix_ref, wet_ref, o_ref, ratio_ref):
    levels = mix_ref.shape[0]
    shape = mix_ref.shape[1:]
    comps = prov_ref.shape[0]

    def below_of(k):
        nxt = jnp.minimum(k + 1, levels - 1)
        middle = 0.5 * (th_ref[k] + th_ref[nxt])
        coupling = mix_ref[k] * wet_ref[k] * wet_ref[nxt] / middle
        return jnp.where(k < levels - 1, coupling, 0.0)

    def forward(k, carry):
        upper, ratio_prev, value_prev = carry
        below = below_of(k)
        depth = th_ref[k]
        diagonal = depth + upper + below
        divisor = diagonal - upper * ratio_prev
        ratio = below / divisor
        ratio_ref[k] = ratio
        values = []
        for c in range(comps):
            value = (depth * prov_ref[c, k] + upper * value_prev[c]) / divisor
            o_ref[c, k] = value
            values.append(value)
        return (below, ratio, tuple(values))

    zeros = jnp.zeros(shape, jnp.float32)
    lax.fori_loop(0, levels, forward, (zeros, zeros, (zeros,) * comps))

    def backward(step, following):
        k = levels - 1 - step
        ratio = ratio_ref[k]
        results = []
        for c in range(comps):
            result = o_ref[c, k] + ratio * following[c]
            o_ref[c, k] = result
            results.append(result)
        return tuple(results)

    lax.fori_loop(0, levels, backward, (zeros,) * comps)


def solve_columns(provisional, mixing, wet_mask, thickness):
    return pl.pallas_call(
        solve_kernel,
        out_shape=jax.ShapeDtypeStruct(provisional.shape, jnp.float32),
        in_specs=[pl.BlockSpec(memory_space=pltpu.SMEM)]
        + [pl.BlockSpec(memory_space=pltpu.VMEM)] * 3,
        out_specs=pl.BlockSpec(memory_space=pltpu.VMEM),
        scratch_shapes=[pltpu.VMEM(mixing.shape, jnp.float32)],
    )(thickness, provisional, mixing, wet_mask)


def solution(mesh):
    return jax.shard_map(
        shards,
        mesh=mesh,
        in_specs=(
            P(None, None, ("gy", "ga"), "gx"),
            P(None, None, ("gy", "ga"), "gx"),
            P(None, ("gy", "ga"), "gx"),
            P(),
            P(("gy", "ga")),
            P(("gy", "ga"), "gx"),
            P(("gy", "ga"), "gx"),
            P(("gy", "ga"), "gx"),
            P(None, ("gy", "ga"), "gx"),
        ),
        out_specs=(
            P(None, None, ("gy", "ga"), "gx"),
            P(None, None, ("gy", "ga"), "gx"),
            P(("gy", "ga"), "gx"),
            P(None, ("gy", "ga"), "gx"),
        ),
        check_vma=False,
    )
```

```python
import jax
import jax.numpy as jnp
from jax import lax
from jax.sharding import PartitionSpec as P
from jax.experimental import pallas as pl
from jax.experimental.pallas import tpu as pltpu

NSUB = 30


step_main = 0.1
visc_four = 0.02
diff_four = 0.02
press_scale = 0.02
step_baro = 0.1
grav_baro = 25.0
expand_temp = 0.2
contract_salt = 0.1


def padded_2(block, sides, width, periodic):
    for axis, dim in sides:
        count = lax.axis_size(axis)
        forward = [(i, i + 1) for i in range(count - 1)]
        if periodic:
            forward.append((count - 1, 0))
        backward = [(target, source) for source, target in forward]
        low = lax.ppermute(
            lax.slice_in_dim(block, block.shape[dim] - width, None, axis=dim), axis, forward
        )
        high = lax.ppermute(lax.slice_in_dim(block, 0, width, axis=dim), axis, backward)
        block = jnp.concatenate([low, block, high], axis=dim)
    return block


def laplace(quantity, wet_mask):
    centre = quantity[..., 1:-1, 1:-1]
    beside_all = (
        quantity[..., 1:-1, 2:]
        + quantity[..., 1:-1, :-2]
        + quantity[..., 2:, 1:-1]
        + quantity[..., :-2, 1:-1]
    )
    return (beside_all - 4.0 * centre) * wet_mask[..., 1:-1, 1:-1]


def diff_x(quantity):
    return 0.5 * (quantity[..., 2:-2, 3:-1] - quantity[..., 2:-2, 1:-3])


def diff_y(quantity):
    return 0.5 * (quantity[..., 3:-1, 2:-2] - quantity[..., 1:-3, 2:-2])


def tendency(padded, pressure, coriolis):
    east_vel = padded[0]
    north_vel = padded[1]
    wet_mask = padded[4]
    inner_wet = wet_mask[..., 2:-2, 2:-2]
    rotate = coriolis[:, None]
    changes = []
    for component in range(4):
        quantity = padded[component]
        advect = diff_x(east_vel * quantity) + diff_y(north_vel * quantity)
        smooth = laplace(laplace(quantity, wet_mask), wet_mask[..., 1:-1, 1:-1])
        if component == 0:
            change = rotate * north_vel[..., 2:-2, 2:-2] - diff_x(pressure) - visc_four * smooth
        elif component == 1:
            change = -rotate * east_vel[..., 2:-2, 2:-2] - diff_y(pressure) - visc_four * smooth
        else:
            change = -diff_four * smooth
        changes.append((change - advect) * inner_wet)
    return jnp.stack(changes)


def vertical_solve(provisional, mixing, wet_mask, thickness):
    levels = thickness.shape[0]
    tail_ones = (1,) * (mixing.ndim - 1)
    depth_col = thickness.reshape((levels,) + tail_ones)
    middle = (0.5 * (thickness[:-1] + thickness[1:])).reshape((levels - 1,) + tail_ones)
    coupling = mixing[:-1] * wet_mask[:-1] * wet_mask[1:] / middle
    zeros_row = jnp.zeros((1,) + mixing.shape[1:], jnp.float32)
    below_link = jnp.concatenate([coupling, zeros_row], axis=0)
    upper_link = jnp.concatenate([zeros_row, coupling], axis=0)
    diagonal = depth_col + upper_link + below_link
    source = depth_col[:, None] * provisional

    def forward(sweep, inputs):
        ratio_prev, value_prev = sweep
        upper_now, diag_now, below_now, source_now = inputs
        divisor = diag_now - upper_now * ratio_prev
        sweep_ratio = below_now / divisor
        sweep_value = (source_now + upper_now[None] * value_prev) / divisor[None]
        return ((sweep_ratio, sweep_value), (sweep_ratio, sweep_value))

    start_sweep = (
        jnp.zeros(mixing.shape[1:], jnp.float32),
        jnp.zeros(provisional.shape[1:], jnp.float32),
    )
    unused, (ratios, values) = lax.scan(
        forward, start_sweep, (upper_link, diagonal, below_link, source)
    )

    def backward(following, inputs):
        sweep_ratio, sweep_value = inputs
        result = sweep_value + sweep_ratio[None] * following
        return (result, result)

    unused_last, solved = lax.scan(
        backward, jnp.zeros(provisional.shape[1:], jnp.float32), (ratios, values), reverse=True
    )
    return solved


def zero_diff(quantity, along):
    extent = quantity.shape[along]
    ahead_part = lax.slice_in_dim(quantity, 1, extent, axis=along)
    behind = lax.slice_in_dim(quantity, 0, extent - 1, axis=along)
    zeros_row = jnp.zeros_like(lax.slice_in_dim(quantity, 0, 1, axis=along))
    return 0.5 * (
        jnp.concatenate([ahead_part, zeros_row], axis=along)
        - jnp.concatenate([zeros_row, behind], axis=along)
    )


def east_zero(quantity):
    return zero_diff(quantity, quantity.ndim - 1)


def north_zero(quantity):
    return zero_diff(quantity, quantity.ndim - 2)


def baro_step(baro_state, statics, east_diff, north_diff):
    height = baro_state[0]
    east_vel = baro_state[1]
    north_vel = baro_state[2]
    depth_ratio = statics[0]
    sea_mask = statics[1]
    rotate = statics[2]
    push_east = statics[3]
    push_north = statics[4]
    new_height = (
        height
        - step_baro * (east_diff(depth_ratio * east_vel) + north_diff(depth_ratio * north_vel))
    ) * sea_mask
    new_east = (
        east_vel + step_baro * (push_east + rotate * north_vel - grav_baro * east_diff(new_height))
    ) * sea_mask
    new_north = (
        north_vel
        + step_baro * (push_north - rotate * east_vel - grav_baro * north_diff(new_height))
    ) * sea_mask
    return jnp.stack([new_height, new_east, new_north])


def zonal_rims(stacked):
    return padded_2(stacked, (("gx", 3),), 2, True)


def merid_rims(stacked):
    return padded_2(stacked, ((("gy", "ga"), 2),), 2, False)


def baro_zonal(operand, halo_width):
    return padded_2(operand, (("gx", 2),), halo_width, True)


def baro_merid_all(operand, halo_width):
    return padded_2(operand, ((("gy", "ga"), 1),), halo_width, False)


def shards(velocity, tracers, mixing, thickness, coriolis, land, bottom, surface, barotropic):
    levels = thickness.shape[0]
    land_f = land.astype(jnp.float32)
    level_ids = lax.broadcasted_iota(jnp.int32, (levels,) + land.shape, 0)
    wet_mask = land_f[None] * (level_ids < bottom[None]).astype(jnp.float32)
    stacked = jnp.concatenate(
        [velocity * wet_mask[None], tracers * wet_mask[None], wet_mask[None]], axis=0
    )
    padded = merid_rims(zonal_rims(stacked))
    depth_col = thickness.reshape((levels, 1, 1))
    weight = (contract_salt * padded[3] - expand_temp * padded[2]) * padded[4] * depth_col
    pressure = press_scale * (jnp.cumsum(weight, axis=0) - weight + 0.5 * weight)
    growth = tendency(padded, pressure, coriolis)
    provisional = stacked[:4] + step_main * growth
    forcing = jnp.sum(depth_col * growth[:2], axis=1)
    depth_sum = jnp.sum(depth_col * wet_mask, axis=0)
    safe_depth = jnp.maximum(depth_sum, 1.0)
    dr = depth_sum / jnp.sum(thickness)
    push_u = forcing[0] / safe_depth * land_f
    push_v = forcing[1] / safe_depth * land_f
    rotate = coriolis[:, None] * jnp.ones_like(land_f)
    fields = jnp.stack([dr, land_f, rotate, push_u, push_v, surface, barotropic[0], barotropic[1]])
    whole = gather_baro(fields)
    rows = land.shape[0]
    row_offset = jnp.full((1,), lax.axis_index(("gy", "ga")) * rows, jnp.int32)
    mine = baro_run(whole, row_offset, land.shape[1])
    average = mine[3:]
    solved = solve_columns(provisional, mixing, wet_mask, thickness)
    thick_col = thickness.reshape((levels, 1, 1))
    depth_mean = jnp.sum(thick_col[None] * wet_mask[None] * solved[:2], axis=1) / safe_depth
    new_velocity = (solved[:2] - depth_mean[:, None] + average[:, None]) * wet_mask[None]
    new_tracers = solved[2:]
    return (new_velocity, new_tracers, mine[0], mine[1:3])


BARO_HALO = 64


def gather_baro(fields):
    count = lax.axis_size("gx")
    forward = [(i, (i + 1) % count) for i in range(count)]
    backward = [(target, source) for source, target in forward]
    low = lax.ppermute(fields[..., -BARO_HALO:], "gx", forward)
    high = lax.ppermute(fields[..., :BARO_HALO], "gx", backward)
    wide = jnp.concatenate([low, fields, high], axis=-1)
    merid = ("gy", "ga")
    parts = lax.axis_size(merid)
    blocks = [wide]
    for shift in range(1, parts):
        pairs = [(d, (d - shift) % parts) for d in range(parts)]
        blocks.append(lax.ppermute(wide, merid, pairs))
    return jnp.stack(blocks)


def baro_kernel(off_ref, f_ref, o_ref):
    parts = f_ref.shape[0]
    block_rows = f_ref.shape[2]
    rows = parts * block_rows
    cols = f_ref.shape[3]

    def field(index):
        return jnp.concatenate([f_ref[part, index] for part in range(parts)], axis=0)

    depth_ratio = field(0)
    sea_mask = field(1)
    rotate = field(2)
    push_east = field(3)
    push_north = field(4)
    offset = off_ref[0]
    last_local = rows - 1 - offset
    first_local = jnp.where(offset == 0, 0, rows - offset)
    row = lax.broadcasted_iota(jnp.int32, (rows, cols), 0)
    not_last = row != last_local
    not_first = row != first_local

    def east_diff(q):
        return 0.5 * (pltpu.roll(q, cols - 1, 1) - pltpu.roll(q, 1, 1))

    def north_diff(q):
        ahead = jnp.where(not_last, pltpu.roll(q, rows - 1, 0), 0.0)
        behind = jnp.where(not_first, pltpu.roll(q, 1, 0), 0.0)
        return 0.5 * (ahead - behind)

    def body(turn, carry):
        height, east_vel, north_vel, sum_east, sum_north = carry
        height = (
            height
            - step_baro * (east_diff(depth_ratio * east_vel) + north_diff(depth_ratio * north_vel))
        ) * sea_mask
        new_east = (
            east_vel + step_baro * (push_east + rotate * north_vel - grav_baro * east_diff(height))
        ) * sea_mask
        new_north = (
            north_vel
            + step_baro * (push_north - rotate * east_vel - grav_baro * north_diff(height))
        ) * sea_mask
        return (height, new_east, new_north, sum_east + new_east, sum_north + new_north)

    zeros = jnp.zeros((rows, cols), jnp.float32)
    carry = (field(5), field(6), field(7), zeros, zeros)
    height, east_vel, north_vel, sum_east, sum_north = lax.fori_loop(0, NSUB, body, carry)
    finals = (height, east_vel, north_vel, sum_east / NSUB, sum_north / NSUB)
    out_cols = o_ref.shape[2]
    for index in range(5):
        o_ref[index] = pltpu.roll(finals[index][:block_rows], cols - BARO_HALO, 1)[:, :out_cols]


def baro_run(whole, row_offset, out_cols):
    return pl.pallas_call(
        baro_kernel,
        out_shape=jax.ShapeDtypeStruct((5, whole.shape[2], out_cols), jnp.float32),
        in_specs=[pl.BlockSpec(memory_space=pltpu.SMEM), pl.BlockSpec(memory_space=pltpu.VMEM)],
        out_specs=pl.BlockSpec(memory_space=pltpu.VMEM),
    )(row_offset, whole)


def solve_kernel(th_ref, prov_ref, mix_ref, wet_ref, o_ref, ratio_ref):
    levels = mix_ref.shape[0]
    shape = mix_ref.shape[1:]
    comps = prov_ref.shape[0]

    def below_of(k):
        nxt = jnp.minimum(k + 1, levels - 1)
        middle = 0.5 * (th_ref[k] + th_ref[nxt])
        coupling = mix_ref[k] * wet_ref[k] * wet_ref[nxt] / middle
        return jnp.where(k < levels - 1, coupling, 0.0)

    def forward(k, carry):
        upper, ratio_prev, value_prev = carry
        below = below_of(k)
        depth = th_ref[k]
        diagonal = depth + upper + below
        divisor = diagonal - upper * ratio_prev
        ratio = below / divisor
        ratio_ref[k] = ratio
        values = []
        for c in range(comps):
            value = (depth * prov_ref[c, k] + upper * value_prev[c]) / divisor
            o_ref[c, k] = value
            values.append(value)
        return (below, ratio, tuple(values))

    zeros = jnp.zeros(shape, jnp.float32)
    lax.fori_loop(0, levels, forward, (zeros, zeros, (zeros,) * comps))

    def backward(step, following):
        k = levels - 1 - step
        ratio = ratio_ref[k]
        results = []
        for c in range(comps):
            result = o_ref[c, k] + ratio * following[c]
            o_ref[c, k] = result
            results.append(result)
        return tuple(results)

    lax.fori_loop(0, levels, backward, (zeros,) * comps)


def solve_columns(provisional, mixing, wet_mask, thickness):
    return pl.pallas_call(
        solve_kernel,
        out_shape=jax.ShapeDtypeStruct(provisional.shape, jnp.float32),
        in_specs=[pl.BlockSpec(memory_space=pltpu.SMEM)]
        + [pl.BlockSpec(memory_space=pltpu.VMEM)] * 3,
        out_specs=pl.BlockSpec(memory_space=pltpu.VMEM),
        scratch_shapes=[pltpu.VMEM(mixing.shape, jnp.float32)],
    )(thickness, provisional, mixing, wet_mask)


def solution(mesh):
    return jax.shard_map(
        shards,
        mesh=mesh,
        in_specs=(
            P(None, None, ("gy", "ga"), "gx"),
            P(None, None, ("gy", "ga"), "gx"),
            P(None, ("gy", "ga"), "gx"),
            P(),
            P(("gy", "ga")),
            P(("gy", "ga"), "gx"),
            P(("gy", "ga"), "gx"),
            P(("gy", "ga"), "gx"),
            P(None, ("gy", "ga"), "gx"),
        ),
        out_specs=(
            P(None, None, ("gy", "ga"), "gx"),
            P(None, None, ("gy", "ga"), "gx"),
            P(("gy", "ga"), "gx"),
            P(None, ("gy", "ga"), "gx"),
        ),
        check_vma=False,
    )
```

```python
import jax
import jax.numpy as jnp
from jax import lax
from jax.sharding import PartitionSpec as P
from jax.experimental import pallas as pl
from jax.experimental.pallas import tpu as pltpu

NSUB = 30


step_main = 0.1
visc_four = 0.02
diff_four = 0.02
press_scale = 0.02
step_baro = 0.1
grav_baro = 25.0
expand_temp = 0.2
contract_salt = 0.1


def laplace(quantity, wet_mask):
    centre = quantity[..., 1:-1, 1:-1]
    beside_all = (
        quantity[..., 1:-1, 2:]
        + quantity[..., 1:-1, :-2]
        + quantity[..., 2:, 1:-1]
        + quantity[..., :-2, 1:-1]
    )
    return (beside_all - 4.0 * centre) * wet_mask[..., 1:-1, 1:-1]


def diff_x(quantity):
    return 0.5 * (quantity[..., 2:-2, 3:-1] - quantity[..., 2:-2, 1:-3])


def diff_y(quantity):
    return 0.5 * (quantity[..., 3:-1, 2:-2] - quantity[..., 1:-3, 2:-2])


def tendency(padded, pressure, coriolis):
    east_vel = padded[0]
    north_vel = padded[1]
    wet_mask = padded[4]
    inner_wet = wet_mask[..., 2:-2, 2:-2]
    rotate = coriolis[:, None]
    changes = []
    for component in range(4):
        quantity = padded[component]
        advect = diff_x(east_vel * quantity) + diff_y(north_vel * quantity)
        smooth = laplace(laplace(quantity, wet_mask), wet_mask[..., 1:-1, 1:-1])
        if component == 0:
            change = rotate * north_vel[..., 2:-2, 2:-2] - diff_x(pressure) - visc_four * smooth
        elif component == 1:
            change = -rotate * east_vel[..., 2:-2, 2:-2] - diff_y(pressure) - visc_four * smooth
        else:
            change = -diff_four * smooth
        changes.append((change - advect) * inner_wet)
    return jnp.stack(changes)


def vertical_solve(provisional, mixing, wet_mask, thickness):
    levels = thickness.shape[0]
    tail_ones = (1,) * (mixing.ndim - 1)
    depth_col = thickness.reshape((levels,) + tail_ones)
    middle = (0.5 * (thickness[:-1] + thickness[1:])).reshape((levels - 1,) + tail_ones)
    coupling = mixing[:-1] * wet_mask[:-1] * wet_mask[1:] / middle
    zeros_row = jnp.zeros((1,) + mixing.shape[1:], jnp.float32)
    below_link = jnp.concatenate([coupling, zeros_row], axis=0)
    upper_link = jnp.concatenate([zeros_row, coupling], axis=0)
    diagonal = depth_col + upper_link + below_link
    source = depth_col[:, None] * provisional

    def forward(sweep, inputs):
        ratio_prev, value_prev = sweep
        upper_now, diag_now, below_now, source_now = inputs
        divisor = diag_now - upper_now * ratio_prev
        sweep_ratio = below_now / divisor
        sweep_value = (source_now + upper_now[None] * value_prev) / divisor[None]
        return ((sweep_ratio, sweep_value), (sweep_ratio, sweep_value))

    start_sweep = (
        jnp.zeros(mixing.shape[1:], jnp.float32),
        jnp.zeros(provisional.shape[1:], jnp.float32),
    )
    unused, (ratios, values) = lax.scan(
        forward, start_sweep, (upper_link, diagonal, below_link, source)
    )

    def backward(following, inputs):
        sweep_ratio, sweep_value = inputs
        result = sweep_value + sweep_ratio[None] * following
        return (result, result)

    unused_last, solved = lax.scan(
        backward, jnp.zeros(provisional.shape[1:], jnp.float32), (ratios, values), reverse=True
    )
    return solved


def zero_diff(quantity, along):
    extent = quantity.shape[along]
    ahead_part = lax.slice_in_dim(quantity, 1, extent, axis=along)
    behind = lax.slice_in_dim(quantity, 0, extent - 1, axis=along)
    zeros_row = jnp.zeros_like(lax.slice_in_dim(quantity, 0, 1, axis=along))
    return 0.5 * (
        jnp.concatenate([ahead_part, zeros_row], axis=along)
        - jnp.concatenate([zeros_row, behind], axis=along)
    )


def east_zero(quantity):
    return zero_diff(quantity, quantity.ndim - 1)


def north_zero(quantity):
    return zero_diff(quantity, quantity.ndim - 2)


def baro_step(baro_state, statics, east_diff, north_diff):
    height = baro_state[0]
    east_vel = baro_state[1]
    north_vel = baro_state[2]
    depth_ratio = statics[0]
    sea_mask = statics[1]
    rotate = statics[2]
    push_east = statics[3]
    push_north = statics[4]
    new_height = (
        height
        - step_baro * (east_diff(depth_ratio * east_vel) + north_diff(depth_ratio * north_vel))
    ) * sea_mask
    new_east = (
        east_vel + step_baro * (push_east + rotate * north_vel - grav_baro * east_diff(new_height))
    ) * sea_mask
    new_north = (
        north_vel
        + step_baro * (push_north - rotate * east_vel - grav_baro * north_diff(new_height))
    ) * sea_mask
    return jnp.stack([new_height, new_east, new_north])


def halo_3d(block):
    zonal = "gx"
    merid = ("gy", "ga")
    both = ("gx", "gy", "ga")
    zonal_n = lax.axis_size(zonal)
    merid_n = lax.axis_size(merid)

    def send(piece, d_zonal, d_merid):
        if d_merid == 0:
            pairs = [(g, (g + d_zonal) % zonal_n) for g in range(zonal_n)]
            return lax.ppermute(piece, zonal, pairs)
        pairs = []
        for g in range(zonal_n):
            for m in range(merid_n):
                target = m + d_merid
                if 0 <= target < merid_n:
                    pairs.append((g * merid_n + m, ((g + d_zonal) % zonal_n) * merid_n + target))
        if d_zonal == 0:
            return lax.ppermute(piece, merid, [(s % merid_n, t % merid_n) for s, t in pairs[:merid_n - 1]])
        return lax.ppermute(piece, both, pairs)

    w = 2
    last_rows = block[..., -w:, :]
    first_rows = block[..., :w, :]
    west = send(block[..., -w:], 1, 0)
    east = send(block[..., :w], -1, 0)
    low = send(last_rows, 0, 1)
    high = send(first_rows, 0, -1)
    low_west = send(last_rows[..., -w:], 1, 1)
    low_east = send(last_rows[..., :w], -1, 1)
    high_west = send(first_rows[..., -w:], 1, -1)
    high_east = send(first_rows[..., :w], -1, -1)
    low_band = jnp.concatenate([low_west, low, low_east], axis=-1)
    middle = jnp.concatenate([west, block, east], axis=-1)
    high_band = jnp.concatenate([high_west, high, high_east], axis=-1)
    return jnp.concatenate([low_band, middle, high_band], axis=-2)


def shards(velocity, tracers, mixing, thickness, coriolis, land, bottom, surface, barotropic):
    levels = thickness.shape[0]
    land_f = land.astype(jnp.float32)
    level_ids = lax.broadcasted_iota(jnp.int32, (levels,) + land.shape, 0)
    wet_mask = land_f[None] * (level_ids < bottom[None]).astype(jnp.float32)
    stacked = jnp.concatenate(
        [velocity * wet_mask[None], tracers * wet_mask[None], wet_mask[None]], axis=0
    )
    padded = halo_3d(stacked)
    depth_col = thickness.reshape((levels, 1, 1))
    weight = (contract_salt * padded[3] - expand_temp * padded[2]) * padded[4] * depth_col
    pressure = press_scale * (jnp.cumsum(weight, axis=0) - weight + 0.5 * weight)
    growth = tendency(padded, pressure, coriolis)
    provisional = stacked[:4] + step_main * growth
    forcing = jnp.sum(depth_col * growth[:2], axis=1)
    depth_sum = jnp.sum(depth_col * wet_mask, axis=0)
    safe_depth = jnp.maximum(depth_sum, 1.0)
    dr = depth_sum / jnp.sum(thickness)
    push_u = forcing[0] / safe_depth * land_f
    push_v = forcing[1] / safe_depth * land_f
    rotate = coriolis[:, None] * jnp.ones_like(land_f)
    fields = jnp.stack([dr, land_f, rotate, push_u, push_v, surface, barotropic[0], barotropic[1]])
    whole = gather_baro(fields)
    rows = land.shape[0]
    row_offset = jnp.full((1,), lax.axis_index(("gy", "ga")) * rows, jnp.int32)
    mine = baro_run(whole, row_offset, land.shape[1])
    average = mine[3:]
    solved = solve_columns(provisional, mixing, wet_mask, thickness)
    thick_col = thickness.reshape((levels, 1, 1))
    depth_mean = jnp.sum(thick_col[None] * wet_mask[None] * solved[:2], axis=1) / safe_depth
    new_velocity = (solved[:2] - depth_mean[:, None] + average[:, None]) * wet_mask[None]
    new_tracers = solved[2:]
    return (new_velocity, new_tracers, mine[0], mine[1:3])


BARO_HALO = 64


def gather_baro(fields):
    count = lax.axis_size("gx")
    forward = [(i, (i + 1) % count) for i in range(count)]
    backward = [(target, source) for source, target in forward]
    low = lax.ppermute(fields[..., -BARO_HALO:], "gx", forward)
    high = lax.ppermute(fields[..., :BARO_HALO], "gx", backward)
    wide = jnp.concatenate([low, fields, high], axis=-1)
    merid = ("gy", "ga")
    parts = lax.axis_size(merid)
    blocks = [wide]
    for shift in range(1, parts):
        pairs = [(d, (d - shift) % parts) for d in range(parts)]
        blocks.append(lax.ppermute(wide, merid, pairs))
    return jnp.stack(blocks)


def baro_kernel(off_ref, f_ref, o_ref):
    parts = f_ref.shape[0]
    block_rows = f_ref.shape[2]
    rows = parts * block_rows
    cols = f_ref.shape[3]

    def field(index):
        return jnp.concatenate([f_ref[part, index] for part in range(parts)], axis=0)

    depth_ratio = field(0)
    sea_mask = field(1)
    rotate = field(2)
    push_east = field(3)
    push_north = field(4)
    offset = off_ref[0]
    last_local = rows - 1 - offset
    first_local = jnp.where(offset == 0, 0, rows - offset)
    row = lax.broadcasted_iota(jnp.int32, (rows, cols), 0)
    not_last = row != last_local
    not_first = row != first_local

    def east_diff(q):
        return 0.5 * (pltpu.roll(q, cols - 1, 1) - pltpu.roll(q, 1, 1))

    def north_diff(q):
        ahead = jnp.where(not_last, pltpu.roll(q, rows - 1, 0), 0.0)
        behind = jnp.where(not_first, pltpu.roll(q, 1, 0), 0.0)
        return 0.5 * (ahead - behind)

    def body(turn, carry):
        height, east_vel, north_vel, sum_east, sum_north = carry
        height = (
            height
            - step_baro * (east_diff(depth_ratio * east_vel) + north_diff(depth_ratio * north_vel))
        ) * sea_mask
        new_east = (
            east_vel + step_baro * (push_east + rotate * north_vel - grav_baro * east_diff(height))
        ) * sea_mask
        new_north = (
            north_vel
            + step_baro * (push_north - rotate * east_vel - grav_baro * north_diff(height))
        ) * sea_mask
        return (height, new_east, new_north, sum_east + new_east, sum_north + new_north)

    zeros = jnp.zeros((rows, cols), jnp.float32)
    carry = (field(5), field(6), field(7), zeros, zeros)
    height, east_vel, north_vel, sum_east, sum_north = lax.fori_loop(0, NSUB, body, carry)
    finals = (height, east_vel, north_vel, sum_east / NSUB, sum_north / NSUB)
    out_cols = o_ref.shape[2]
    for index in range(5):
        o_ref[index] = pltpu.roll(finals[index][:block_rows], cols - BARO_HALO, 1)[:, :out_cols]


def baro_run(whole, row_offset, out_cols):
    return pl.pallas_call(
        baro_kernel,
        out_shape=jax.ShapeDtypeStruct((5, whole.shape[2], out_cols), jnp.float32),
        in_specs=[pl.BlockSpec(memory_space=pltpu.SMEM), pl.BlockSpec(memory_space=pltpu.VMEM)],
        out_specs=pl.BlockSpec(memory_space=pltpu.VMEM),
    )(row_offset, whole)


def solve_kernel(th_ref, prov_ref, mix_ref, wet_ref, o_ref, ratio_ref):
    levels = mix_ref.shape[0]
    shape = mix_ref.shape[1:]
    comps = prov_ref.shape[0]

    def below_of(k):
        nxt = jnp.minimum(k + 1, levels - 1)
        middle = 0.5 * (th_ref[k] + th_ref[nxt])
        coupling = mix_ref[k] * wet_ref[k] * wet_ref[nxt] / middle
        return jnp.where(k < levels - 1, coupling, 0.0)

    def forward(k, carry):
        upper, ratio_prev, value_prev = carry
        below = below_of(k)
        depth = th_ref[k]
        diagonal = depth + upper + below
        divisor = diagonal - upper * ratio_prev
        ratio = below / divisor
        ratio_ref[k] = ratio
        values = []
        for c in range(comps):
            value = (depth * prov_ref[c, k] + upper * value_prev[c]) / divisor
            o_ref[c, k] = value
            values.append(value)
        return (below, ratio, tuple(values))

    zeros = jnp.zeros(shape, jnp.float32)
    lax.fori_loop(0, levels, forward, (zeros, zeros, (zeros,) * comps))

    def backward(step, following):
        k = levels - 1 - step
        ratio = ratio_ref[k]
        results = []
        for c in range(comps):
            result = o_ref[c, k] + ratio * following[c]
            o_ref[c, k] = result
            results.append(result)
        return tuple(results)

    lax.fori_loop(0, levels, backward, (zeros,) * comps)


def solve_columns(provisional, mixing, wet_mask, thickness):
    return pl.pallas_call(
        solve_kernel,
        out_shape=jax.ShapeDtypeStruct(provisional.shape, jnp.float32),
        in_specs=[pl.BlockSpec(memory_space=pltpu.SMEM)]
        + [pl.BlockSpec(memory_space=pltpu.VMEM)] * 3,
        out_specs=pl.BlockSpec(memory_space=pltpu.VMEM),
        scratch_shapes=[pltpu.VMEM(mixing.shape, jnp.float32)],
    )(thickness, provisional, mixing, wet_mask)


def solution(mesh):
    return jax.shard_map(
        shards,
        mesh=mesh,
        in_specs=(
            P(None, None, ("gy", "ga"), "gx"),
            P(None, None, ("gy", "ga"), "gx"),
            P(None, ("gy", "ga"), "gx"),
            P(),
            P(("gy", "ga")),
            P(("gy", "ga"), "gx"),
            P(("gy", "ga"), "gx"),
            P(("gy", "ga"), "gx"),
            P(None, ("gy", "ga"), "gx"),
        ),
        out_specs=(
            P(None, None, ("gy", "ga"), "gx"),
            P(None, None, ("gy", "ga"), "gx"),
            P(("gy", "ga"), "gx"),
            P(None, ("gy", "ga"), "gx"),
        ),
        check_vma=False,
    )
```

```python
import jax
import jax.numpy as jnp
from jax import lax
from jax.sharding import PartitionSpec as P
from jax.experimental import pallas as pl
from jax.experimental.pallas import tpu as pltpu

NSUB = 30


step_main = 0.1
visc_four = 0.02
diff_four = 0.02
press_scale = 0.02
step_baro = 0.1
grav_baro = 25.0
expand_temp = 0.2
contract_salt = 0.1


def laplace(quantity, wet_mask):
    centre = quantity[..., 1:-1, 1:-1]
    beside_all = (
        quantity[..., 1:-1, 2:]
        + quantity[..., 1:-1, :-2]
        + quantity[..., 2:, 1:-1]
        + quantity[..., :-2, 1:-1]
    )
    return (beside_all - 4.0 * centre) * wet_mask[..., 1:-1, 1:-1]


def diff_x(quantity):
    return 0.5 * (quantity[..., 2:-2, 3:-1] - quantity[..., 2:-2, 1:-3])


def diff_y(quantity):
    return 0.5 * (quantity[..., 3:-1, 2:-2] - quantity[..., 1:-3, 2:-2])


def tendency(padded, pressure, coriolis):
    east_vel = padded[0]
    north_vel = padded[1]
    wet_mask = padded[4]
    inner_wet = wet_mask[..., 2:-2, 2:-2]
    rotate = coriolis[:, None]
    changes = []
    for component in range(4):
        quantity = padded[component]
        advect = diff_x(east_vel * quantity) + diff_y(north_vel * quantity)
        smooth = laplace(laplace(quantity, wet_mask), wet_mask[..., 1:-1, 1:-1])
        if component == 0:
            change = rotate * north_vel[..., 2:-2, 2:-2] - diff_x(pressure) - visc_four * smooth
        elif component == 1:
            change = -rotate * east_vel[..., 2:-2, 2:-2] - diff_y(pressure) - visc_four * smooth
        else:
            change = -diff_four * smooth
        changes.append((change - advect) * inner_wet)
    return jnp.stack(changes)


def vertical_solve(provisional, mixing, wet_mask, thickness):
    levels = thickness.shape[0]
    tail_ones = (1,) * (mixing.ndim - 1)
    depth_col = thickness.reshape((levels,) + tail_ones)
    middle = (0.5 * (thickness[:-1] + thickness[1:])).reshape((levels - 1,) + tail_ones)
    coupling = mixing[:-1] * wet_mask[:-1] * wet_mask[1:] / middle
    zeros_row = jnp.zeros((1,) + mixing.shape[1:], jnp.float32)
    below_link = jnp.concatenate([coupling, zeros_row], axis=0)
    upper_link = jnp.concatenate([zeros_row, coupling], axis=0)
    diagonal = depth_col + upper_link + below_link
    source = depth_col[:, None] * provisional

    def forward(sweep, inputs):
        ratio_prev, value_prev = sweep
        upper_now, diag_now, below_now, source_now = inputs
        divisor = diag_now - upper_now * ratio_prev
        sweep_ratio = below_now / divisor
        sweep_value = (source_now + upper_now[None] * value_prev) / divisor[None]
        return ((sweep_ratio, sweep_value), (sweep_ratio, sweep_value))

    start_sweep = (
        jnp.zeros(mixing.shape[1:], jnp.float32),
        jnp.zeros(provisional.shape[1:], jnp.float32),
    )
    unused, (ratios, values) = lax.scan(
        forward, start_sweep, (upper_link, diagonal, below_link, source)
    )

    def backward(following, inputs):
        sweep_ratio, sweep_value = inputs
        result = sweep_value + sweep_ratio[None] * following
        return (result, result)

    unused_last, solved = lax.scan(
        backward, jnp.zeros(provisional.shape[1:], jnp.float32), (ratios, values), reverse=True
    )
    return solved


def zero_diff(quantity, along):
    extent = quantity.shape[along]
    ahead_part = lax.slice_in_dim(quantity, 1, extent, axis=along)
    behind = lax.slice_in_dim(quantity, 0, extent - 1, axis=along)
    zeros_row = jnp.zeros_like(lax.slice_in_dim(quantity, 0, 1, axis=along))
    return 0.5 * (
        jnp.concatenate([ahead_part, zeros_row], axis=along)
        - jnp.concatenate([zeros_row, behind], axis=along)
    )


def east_zero(quantity):
    return zero_diff(quantity, quantity.ndim - 1)


def north_zero(quantity):
    return zero_diff(quantity, quantity.ndim - 2)


def baro_step(baro_state, statics, east_diff, north_diff):
    height = baro_state[0]
    east_vel = baro_state[1]
    north_vel = baro_state[2]
    depth_ratio = statics[0]
    sea_mask = statics[1]
    rotate = statics[2]
    push_east = statics[3]
    push_north = statics[4]
    new_height = (
        height
        - step_baro * (east_diff(depth_ratio * east_vel) + north_diff(depth_ratio * north_vel))
    ) * sea_mask
    new_east = (
        east_vel + step_baro * (push_east + rotate * north_vel - grav_baro * east_diff(new_height))
    ) * sea_mask
    new_north = (
        north_vel
        + step_baro * (push_north - rotate * east_vel - grav_baro * north_diff(new_height))
    ) * sea_mask
    return jnp.stack([new_height, new_east, new_north])


def halo_3d(block):
    zonal = "gx"
    merid = ("gy", "ga")
    both = ("gx", "gy", "ga")
    zonal_n = lax.axis_size(zonal)
    merid_n = lax.axis_size(merid)

    def send(piece, d_zonal, d_merid):
        if d_merid == 0:
            pairs = [(g, (g + d_zonal) % zonal_n) for g in range(zonal_n)]
            return lax.ppermute(piece, zonal, pairs)
        pairs = []
        for g in range(zonal_n):
            for m in range(merid_n):
                target = m + d_merid
                if 0 <= target < merid_n:
                    pairs.append((g * merid_n + m, ((g + d_zonal) % zonal_n) * merid_n + target))
        if d_zonal == 0:
            return lax.ppermute(piece, merid, [(s % merid_n, t % merid_n) for s, t in pairs[:merid_n - 1]])
        return lax.ppermute(piece, both, pairs)

    w = 2
    last_rows = block[..., -w:, :]
    first_rows = block[..., :w, :]
    west = send(block[..., -w:], 1, 0)
    east = send(block[..., :w], -1, 0)
    low = send(last_rows, 0, 1)
    high = send(first_rows, 0, -1)
    low_west = send(last_rows[..., -w:], 1, 1)
    low_east = send(last_rows[..., :w], -1, 1)
    high_west = send(first_rows[..., -w:], 1, -1)
    high_east = send(first_rows[..., :w], -1, -1)
    low_band = jnp.concatenate([low_west, low, low_east], axis=-1)
    middle = jnp.concatenate([west, block, east], axis=-1)
    high_band = jnp.concatenate([high_west, high, high_east], axis=-1)
    return jnp.concatenate([low_band, middle, high_band], axis=-2)


def shards(velocity, tracers, mixing, thickness, coriolis, land, bottom, surface, barotropic):
    levels = thickness.shape[0]
    land_f = land.astype(jnp.float32)
    level_ids = lax.broadcasted_iota(jnp.int32, (levels,) + land.shape, 0)
    wet_mask = land_f[None] * (level_ids < bottom[None]).astype(jnp.float32)
    stacked = jnp.concatenate(
        [velocity * wet_mask[None], tracers * wet_mask[None], wet_mask[None]], axis=0
    )
    padded = halo_3d(stacked)
    depth_col = thickness.reshape((levels, 1, 1))
    weight = (contract_salt * padded[3] - expand_temp * padded[2]) * padded[4] * depth_col
    pressure = press_scale * (jnp.cumsum(weight, axis=0) - weight + 0.5 * weight)
    growth = tendency(padded, pressure, coriolis)
    provisional = stacked[:4] + step_main * growth
    forcing = jnp.sum(depth_col * growth[:2], axis=1)
    depth_sum = jnp.sum(depth_col * wet_mask, axis=0)
    safe_depth = jnp.maximum(depth_sum, 1.0)
    dr = depth_sum / jnp.sum(thickness)
    push_u = forcing[0] / safe_depth * land_f
    push_v = forcing[1] / safe_depth * land_f
    rotate = coriolis[:, None] * jnp.ones_like(land_f)
    fields = jnp.stack([dr, land_f, rotate, push_u, push_v, surface, barotropic[0], barotropic[1]])
    whole = gather_baro(fields)
    rows = land.shape[0]
    row_offset = jnp.full((1,), lax.axis_index(("gy", "ga")) * rows, jnp.int32)
    mine = baro_run(whole, row_offset, land.shape[1])
    average = mine[3:]
    solved = solve_columns(provisional, mixing, wet_mask, thickness)
    thick_col = thickness.reshape((levels, 1, 1))
    depth_mean = jnp.sum(thick_col[None] * wet_mask[None] * solved[:2], axis=1) / safe_depth
    new_velocity = (solved[:2] - depth_mean[:, None] + average[:, None]) * wet_mask[None]
    new_tracers = solved[2:]
    return (new_velocity, new_tracers, mine[0], mine[1:3])


BARO_HALO = 64


def gather_baro(fields):
    count = lax.axis_size("gx")
    forward = [(i, (i + 1) % count) for i in range(count)]
    backward = [(target, source) for source, target in forward]
    low = lax.ppermute(fields[..., -BARO_HALO:], "gx", forward)
    high = lax.ppermute(fields[..., :BARO_HALO], "gx", backward)
    wide = jnp.concatenate([low, fields, high], axis=-1)
    merid = ("gy", "ga")
    parts = lax.axis_size(merid)
    copies = jnp.broadcast_to(wide[None], (parts,) + wide.shape)
    return lax.all_to_all(copies, merid, 0, 0)


def baro_kernel(off_ref, f_ref, o_ref, keep_ref):
    parts = f_ref.shape[0]
    block_rows = f_ref.shape[2]
    rows = parts * block_rows
    cols = f_ref.shape[3]

    def field(index):
        return jnp.concatenate([f_ref[part, index] for part in range(parts)], axis=0)

    depth_ratio = field(0)
    sea_mask = field(1)
    rotate = field(2)
    push_east = field(3)
    push_north = field(4)
    row = lax.broadcasted_iota(jnp.int32, (rows, cols), 0)
    not_last = row != rows - 1
    not_first = row != 0

    def east_diff(q):
        return 0.5 * (pltpu.roll(q, cols - 1, 1) - pltpu.roll(q, 1, 1))

    def north_diff(q):
        ahead = jnp.where(not_last, pltpu.roll(q, rows - 1, 0), 0.0)
        behind = jnp.where(not_first, pltpu.roll(q, 1, 0), 0.0)
        return 0.5 * (ahead - behind)

    def body(turn, carry):
        height, east_vel, north_vel, sum_east, sum_north = carry
        height = (
            height
            - step_baro * (east_diff(depth_ratio * east_vel) + north_diff(depth_ratio * north_vel))
        ) * sea_mask
        new_east = (
            east_vel + step_baro * (push_east + rotate * north_vel - grav_baro * east_diff(height))
        ) * sea_mask
        new_north = (
            north_vel
            + step_baro * (push_north - rotate * east_vel - grav_baro * north_diff(height))
        ) * sea_mask
        return (height, new_east, new_north, sum_east + new_east, sum_north + new_north)

    zeros = jnp.zeros((rows, cols), jnp.float32)
    carry = (field(5), field(6), field(7), zeros, zeros)
    height, east_vel, north_vel, sum_east, sum_north = lax.fori_loop(0, NSUB, body, carry)
    finals = (height, east_vel, north_vel, sum_east / NSUB, sum_north / NSUB)
    out_cols = o_ref.shape[2]
    start = pl.multiple_of(off_ref[0], block_rows)
    for index in range(5):
        keep_ref[...] = pltpu.roll(finals[index], cols - BARO_HALO, 1)
        o_ref[index] = keep_ref[pl.ds(start, block_rows), :out_cols]


def baro_run(whole, row_offset, out_cols):
    return pl.pallas_call(
        baro_kernel,
        out_shape=jax.ShapeDtypeStruct((5, whole.shape[2], out_cols), jnp.float32),
        in_specs=[pl.BlockSpec(memory_space=pltpu.SMEM), pl.BlockSpec(memory_space=pltpu.VMEM)],
        out_specs=pl.BlockSpec(memory_space=pltpu.VMEM),
        scratch_shapes=[pltpu.VMEM((whole.shape[0] * whole.shape[2], whole.shape[3]), jnp.float32)],
    )(row_offset, whole)


def solve_kernel(th_ref, prov_ref, mix_ref, wet_ref, o_ref, ratio_ref):
    levels = mix_ref.shape[0]
    shape = mix_ref.shape[1:]
    comps = prov_ref.shape[0]

    def below_of(k):
        nxt = jnp.minimum(k + 1, levels - 1)
        middle = 0.5 * (th_ref[k] + th_ref[nxt])
        coupling = mix_ref[k] * wet_ref[k] * wet_ref[nxt] / middle
        return jnp.where(k < levels - 1, coupling, 0.0)

    def forward(k, carry):
        upper, ratio_prev, value_prev = carry
        below = below_of(k)
        depth = th_ref[k]
        diagonal = depth + upper + below
        divisor = diagonal - upper * ratio_prev
        ratio = below / divisor
        ratio_ref[k] = ratio
        values = []
        for c in range(comps):
            value = (depth * prov_ref[c, k] + upper * value_prev[c]) / divisor
            o_ref[c, k] = value
            values.append(value)
        return (below, ratio, tuple(values))

    zeros = jnp.zeros(shape, jnp.float32)
    lax.fori_loop(0, levels, forward, (zeros, zeros, (zeros,) * comps))

    def backward(step, following):
        k = levels - 1 - step
        ratio = ratio_ref[k]
        results = []
        for c in range(comps):
            result = o_ref[c, k] + ratio * following[c]
            o_ref[c, k] = result
            results.append(result)
        return tuple(results)

    lax.fori_loop(0, levels, backward, (zeros,) * comps)


def solve_columns(provisional, mixing, wet_mask, thickness):
    return pl.pallas_call(
        solve_kernel,
        out_shape=jax.ShapeDtypeStruct(provisional.shape, jnp.float32),
        in_specs=[pl.BlockSpec(memory_space=pltpu.SMEM)]
        + [pl.BlockSpec(memory_space=pltpu.VMEM)] * 3,
        out_specs=pl.BlockSpec(memory_space=pltpu.VMEM),
        scratch_shapes=[pltpu.VMEM(mixing.shape, jnp.float32)],
    )(thickness, provisional, mixing, wet_mask)


def solution(mesh):
    return jax.shard_map(
        shards,
        mesh=mesh,
        in_specs=(
            P(None, None, ("gy", "ga"), "gx"),
            P(None, None, ("gy", "ga"), "gx"),
            P(None, ("gy", "ga"), "gx"),
            P(),
            P(("gy", "ga")),
            P(("gy", "ga"), "gx"),
            P(("gy", "ga"), "gx"),
            P(("gy", "ga"), "gx"),
            P(None, ("gy", "ga"), "gx"),
        ),
        out_specs=(
            P(None, None, ("gy", "ga"), "gx"),
            P(None, None, ("gy", "ga"), "gx"),
            P(("gy", "ga"), "gx"),
            P(None, ("gy", "ga"), "gx"),
        ),
        check_vma=False,
    )
```

```python
import jax
import jax.numpy as jnp
from jax import lax
from jax.sharding import PartitionSpec as P
from jax.experimental import pallas as pl
from jax.experimental.pallas import tpu as pltpu

NSUB = 30


step_main = 0.1
visc_four = 0.02
diff_four = 0.02
press_scale = 0.02
step_baro = 0.1
grav_baro = 25.0
expand_temp = 0.2
contract_salt = 0.1


def laplace(quantity, wet_mask):
    centre = quantity[..., 1:-1, 1:-1]
    beside_all = (
        quantity[..., 1:-1, 2:]
        + quantity[..., 1:-1, :-2]
        + quantity[..., 2:, 1:-1]
        + quantity[..., :-2, 1:-1]
    )
    return (beside_all - 4.0 * centre) * wet_mask[..., 1:-1, 1:-1]


def diff_x(quantity):
    return 0.5 * (quantity[..., 2:-2, 3:-1] - quantity[..., 2:-2, 1:-3])


def diff_y(quantity):
    return 0.5 * (quantity[..., 3:-1, 2:-2] - quantity[..., 1:-3, 2:-2])


def tendency(padded, pressure, coriolis):
    east_vel = padded[0]
    north_vel = padded[1]
    wet_mask = padded[4]
    inner_wet = wet_mask[..., 2:-2, 2:-2]
    rotate = coriolis[:, None]
    changes = []
    for component in range(4):
        quantity = padded[component]
        advect = diff_x(east_vel * quantity) + diff_y(north_vel * quantity)
        smooth = laplace(laplace(quantity, wet_mask), wet_mask[..., 1:-1, 1:-1])
        if component == 0:
            change = rotate * north_vel[..., 2:-2, 2:-2] - diff_x(pressure) - visc_four * smooth
        elif component == 1:
            change = -rotate * east_vel[..., 2:-2, 2:-2] - diff_y(pressure) - visc_four * smooth
        else:
            change = -diff_four * smooth
        changes.append((change - advect) * inner_wet)
    return jnp.stack(changes)


def vertical_solve(provisional, mixing, wet_mask, thickness):
    levels = thickness.shape[0]
    tail_ones = (1,) * (mixing.ndim - 1)
    depth_col = thickness.reshape((levels,) + tail_ones)
    middle = (0.5 * (thickness[:-1] + thickness[1:])).reshape((levels - 1,) + tail_ones)
    coupling = mixing[:-1] * wet_mask[:-1] * wet_mask[1:] / middle
    zeros_row = jnp.zeros((1,) + mixing.shape[1:], jnp.float32)
    below_link = jnp.concatenate([coupling, zeros_row], axis=0)
    upper_link = jnp.concatenate([zeros_row, coupling], axis=0)
    diagonal = depth_col + upper_link + below_link
    source = depth_col[:, None] * provisional

    def forward(sweep, inputs):
        ratio_prev, value_prev = sweep
        upper_now, diag_now, below_now, source_now = inputs
        divisor = diag_now - upper_now * ratio_prev
        sweep_ratio = below_now / divisor
        sweep_value = (source_now + upper_now[None] * value_prev) / divisor[None]
        return ((sweep_ratio, sweep_value), (sweep_ratio, sweep_value))

    start_sweep = (
        jnp.zeros(mixing.shape[1:], jnp.float32),
        jnp.zeros(provisional.shape[1:], jnp.float32),
    )
    unused, (ratios, values) = lax.scan(
        forward, start_sweep, (upper_link, diagonal, below_link, source)
    )

    def backward(following, inputs):
        sweep_ratio, sweep_value = inputs
        result = sweep_value + sweep_ratio[None] * following
        return (result, result)

    unused_last, solved = lax.scan(
        backward, jnp.zeros(provisional.shape[1:], jnp.float32), (ratios, values), reverse=True
    )
    return solved


def zero_diff(quantity, along):
    extent = quantity.shape[along]
    ahead_part = lax.slice_in_dim(quantity, 1, extent, axis=along)
    behind = lax.slice_in_dim(quantity, 0, extent - 1, axis=along)
    zeros_row = jnp.zeros_like(lax.slice_in_dim(quantity, 0, 1, axis=along))
    return 0.5 * (
        jnp.concatenate([ahead_part, zeros_row], axis=along)
        - jnp.concatenate([zeros_row, behind], axis=along)
    )


def east_zero(quantity):
    return zero_diff(quantity, quantity.ndim - 1)


def north_zero(quantity):
    return zero_diff(quantity, quantity.ndim - 2)


def baro_step(baro_state, statics, east_diff, north_diff):
    height = baro_state[0]
    east_vel = baro_state[1]
    north_vel = baro_state[2]
    depth_ratio = statics[0]
    sea_mask = statics[1]
    rotate = statics[2]
    push_east = statics[3]
    push_north = statics[4]
    new_height = (
        height
        - step_baro * (east_diff(depth_ratio * east_vel) + north_diff(depth_ratio * north_vel))
    ) * sea_mask
    new_east = (
        east_vel + step_baro * (push_east + rotate * north_vel - grav_baro * east_diff(new_height))
    ) * sea_mask
    new_north = (
        north_vel
        + step_baro * (push_north - rotate * east_vel - grav_baro * north_diff(new_height))
    ) * sea_mask
    return jnp.stack([new_height, new_east, new_north])


def halo_3d(block):
    zonal = "gx"
    merid = ("gy", "ga")
    both = ("gx", "gy", "ga")
    zonal_n = lax.axis_size(zonal)
    merid_n = lax.axis_size(merid)

    def send(piece, d_zonal, d_merid):
        if d_merid == 0:
            pairs = [(g, (g + d_zonal) % zonal_n) for g in range(zonal_n)]
            return lax.ppermute(piece, zonal, pairs)
        pairs = []
        for g in range(zonal_n):
            for m in range(merid_n):
                target = m + d_merid
                if 0 <= target < merid_n:
                    pairs.append((g * merid_n + m, ((g + d_zonal) % zonal_n) * merid_n + target))
        if d_zonal == 0:
            return lax.ppermute(piece, merid, [(s % merid_n, t % merid_n) for s, t in pairs[:merid_n - 1]])
        return lax.ppermute(piece, both, pairs)

    w = 2
    last_rows = block[..., -w:, :]
    first_rows = block[..., :w, :]
    west = send(block[..., -w:], 1, 0)
    east = send(block[..., :w], -1, 0)
    low = send(last_rows, 0, 1)
    high = send(first_rows, 0, -1)
    low_west = send(last_rows[..., -w:], 1, 1)
    low_east = send(last_rows[..., :w], -1, 1)
    high_west = send(first_rows[..., -w:], 1, -1)
    high_east = send(first_rows[..., :w], -1, -1)
    low_band = jnp.concatenate([low_west, low, low_east], axis=-1)
    middle = jnp.concatenate([west, block, east], axis=-1)
    high_band = jnp.concatenate([high_west, high, high_east], axis=-1)
    return jnp.concatenate([low_band, middle, high_band], axis=-2)


def shards(velocity, tracers, mixing, thickness, coriolis, land, bottom, surface, barotropic):
    levels = thickness.shape[0]
    land_f = land.astype(jnp.float32)
    level_ids = lax.broadcasted_iota(jnp.int32, (levels,) + land.shape, 0)
    wet_mask = land_f[None] * (level_ids < bottom[None]).astype(jnp.float32)
    stacked = jnp.concatenate(
        [velocity * wet_mask[None], tracers * wet_mask[None], wet_mask[None]], axis=0
    )
    padded = halo_3d(stacked)
    depth_col = thickness.reshape((levels, 1, 1))
    pressure = pressure_run(thickness, padded)
    growth = tendency(padded, pressure, coriolis)
    provisional = stacked[:4] + step_main * growth
    forcing = jnp.sum(depth_col * growth[:2], axis=1)
    depth_sum = jnp.sum(depth_col * wet_mask, axis=0)
    safe_depth = jnp.maximum(depth_sum, 1.0)
    dr = depth_sum / jnp.sum(thickness)
    push_u = forcing[0] / safe_depth * land_f
    push_v = forcing[1] / safe_depth * land_f
    rotate = coriolis[:, None] * jnp.ones_like(land_f)
    fields = jnp.stack([dr, land_f, rotate, push_u, push_v, surface, barotropic[0], barotropic[1]])
    whole = gather_baro(fields)
    rows = land.shape[0]
    row_offset = jnp.full((1,), lax.axis_index(("gy", "ga")) * rows, jnp.int32)
    mine = baro_run(whole, row_offset, land.shape[1])
    average = mine[3:]
    solved = solve_columns(provisional, mixing, wet_mask, thickness)
    thick_col = thickness.reshape((levels, 1, 1))
    depth_mean = jnp.sum(thick_col[None] * wet_mask[None] * solved[:2], axis=1) / safe_depth
    new_velocity = (solved[:2] - depth_mean[:, None] + average[:, None]) * wet_mask[None]
    new_tracers = solved[2:]
    return (new_velocity, new_tracers, mine[0], mine[1:3])


BARO_HALO = 64


def gather_baro(fields):
    count = lax.axis_size("gx")
    forward = [(i, (i + 1) % count) for i in range(count)]
    backward = [(target, source) for source, target in forward]
    low = lax.ppermute(fields[..., -BARO_HALO:], "gx", forward)
    high = lax.ppermute(fields[..., :BARO_HALO], "gx", backward)
    wide = jnp.concatenate([low, fields, high], axis=-1)
    merid = ("gy", "ga")
    parts = lax.axis_size(merid)
    blocks = [wide]
    for shift in range(1, parts):
        pairs = [(d, (d - shift) % parts) for d in range(parts)]
        blocks.append(lax.ppermute(wide, merid, pairs))
    return jnp.stack(blocks)


def baro_kernel(off_ref, f_ref, o_ref):
    parts = f_ref.shape[0]
    block_rows = f_ref.shape[2]
    rows = parts * block_rows
    cols = f_ref.shape[3]

    def field(index):
        return jnp.concatenate([f_ref[part, index] for part in range(parts)], axis=0)

    depth_ratio = field(0)
    sea_mask = field(1)
    rotate = field(2)
    push_east = field(3)
    push_north = field(4)
    offset = off_ref[0]
    last_local = rows - 1 - offset
    first_local = jnp.where(offset == 0, 0, rows - offset)
    row = lax.broadcasted_iota(jnp.int32, (rows, cols), 0)
    not_last = row != last_local
    not_first = row != first_local

    def east_diff(q):
        return 0.5 * (pltpu.roll(q, cols - 1, 1) - pltpu.roll(q, 1, 1))

    def north_diff(q):
        ahead = jnp.where(not_last, pltpu.roll(q, rows - 1, 0), 0.0)
        behind = jnp.where(not_first, pltpu.roll(q, 1, 0), 0.0)
        return 0.5 * (ahead - behind)

    def body(turn, carry):
        height, east_vel, north_vel, sum_east, sum_north = carry
        height = (
            height
            - step_baro * (east_diff(depth_ratio * east_vel) + north_diff(depth_ratio * north_vel))
        ) * sea_mask
        new_east = (
            east_vel + step_baro * (push_east + rotate * north_vel - grav_baro * east_diff(height))
        ) * sea_mask
        new_north = (
            north_vel
            + step_baro * (push_north - rotate * east_vel - grav_baro * north_diff(height))
        ) * sea_mask
        return (height, new_east, new_north, sum_east + new_east, sum_north + new_north)

    zeros = jnp.zeros((rows, cols), jnp.float32)
    carry = (field(5), field(6), field(7), zeros, zeros)
    height, east_vel, north_vel, sum_east, sum_north = lax.fori_loop(0, NSUB, body, carry)
    finals = (height, east_vel, north_vel, sum_east / NSUB, sum_north / NSUB)
    out_cols = o_ref.shape[2]
    for index in range(5):
        o_ref[index] = pltpu.roll(finals[index][:block_rows], cols - BARO_HALO, 1)[:, :out_cols]


def baro_run(whole, row_offset, out_cols):
    return pl.pallas_call(
        baro_kernel,
        out_shape=jax.ShapeDtypeStruct((5, whole.shape[2], out_cols), jnp.float32),
        in_specs=[pl.BlockSpec(memory_space=pltpu.SMEM), pl.BlockSpec(memory_space=pltpu.VMEM)],
        out_specs=pl.BlockSpec(memory_space=pltpu.VMEM),
    )(row_offset, whole)


def pressure_kernel(th_ref, pad_ref, o_ref):
    levels = pad_ref.shape[1]

    def body(k, overlying):
        weight = (contract_salt * pad_ref[3, k] - expand_temp * pad_ref[2, k]) * pad_ref[4, k] * th_ref[k]
        o_ref[k] = press_scale * (overlying + 0.5 * weight)
        return overlying + weight

    lax.fori_loop(0, levels, body, jnp.zeros(pad_ref.shape[2:], jnp.float32))


def pressure_run(thickness, padded):
    return pl.pallas_call(
        pressure_kernel,
        out_shape=jax.ShapeDtypeStruct(padded.shape[1:], jnp.float32),
        in_specs=[pl.BlockSpec(memory_space=pltpu.SMEM), pl.BlockSpec(memory_space=pltpu.VMEM)],
        out_specs=pl.BlockSpec(memory_space=pltpu.VMEM),
    )(thickness, padded)


def solve_kernel(th_ref, prov_ref, mix_ref, wet_ref, o_ref, ratio_ref):
    levels = mix_ref.shape[0]
    shape = mix_ref.shape[1:]
    comps = prov_ref.shape[0]

    def below_of(k):
        nxt = jnp.minimum(k + 1, levels - 1)
        middle = 0.5 * (th_ref[k] + th_ref[nxt])
        coupling = mix_ref[k] * wet_ref[k] * wet_ref[nxt] / middle
        return jnp.where(k < levels - 1, coupling, 0.0)

    def forward(k, carry):
        upper, ratio_prev, value_prev = carry
        below = below_of(k)
        depth = th_ref[k]
        diagonal = depth + upper + below
        divisor = diagonal - upper * ratio_prev
        ratio = below / divisor
        ratio_ref[k] = ratio
        values = []
        for c in range(comps):
            value = (depth * prov_ref[c, k] + upper * value_prev[c]) / divisor
            o_ref[c, k] = value
            values.append(value)
        return (below, ratio, tuple(values))

    zeros = jnp.zeros(shape, jnp.float32)
    lax.fori_loop(0, levels, forward, (zeros, zeros, (zeros,) * comps))

    def backward(step, following):
        k = levels - 1 - step
        ratio = ratio_ref[k]
        results = []
        for c in range(comps):
            result = o_ref[c, k] + ratio * following[c]
            o_ref[c, k] = result
            results.append(result)
        return tuple(results)

    lax.fori_loop(0, levels, backward, (zeros,) * comps)


def solve_columns(provisional, mixing, wet_mask, thickness):
    return pl.pallas_call(
        solve_kernel,
        out_shape=jax.ShapeDtypeStruct(provisional.shape, jnp.float32),
        in_specs=[pl.BlockSpec(memory_space=pltpu.SMEM)]
        + [pl.BlockSpec(memory_space=pltpu.VMEM)] * 3,
        out_specs=pl.BlockSpec(memory_space=pltpu.VMEM),
        scratch_shapes=[pltpu.VMEM(mixing.shape, jnp.float32)],
    )(thickness, provisional, mixing, wet_mask)


def solution(mesh):
    return jax.shard_map(
        shards,
        mesh=mesh,
        in_specs=(
            P(None, None, ("gy", "ga"), "gx"),
            P(None, None, ("gy", "ga"), "gx"),
            P(None, ("gy", "ga"), "gx"),
            P(),
            P(("gy", "ga")),
            P(("gy", "ga"), "gx"),
            P(("gy", "ga"), "gx"),
            P(("gy", "ga"), "gx"),
            P(None, ("gy", "ga"), "gx"),
        ),
        out_specs=(
            P(None, None, ("gy", "ga"), "gx"),
            P(None, None, ("gy", "ga"), "gx"),
            P(("gy", "ga"), "gx"),
            P(None, ("gy", "ga"), "gx"),
        ),
        check_vma=False,
    )
```

```python
import jax
import jax.numpy as jnp
from jax import lax
from jax.sharding import PartitionSpec as P
from jax.experimental import pallas as pl
from jax.experimental.pallas import tpu as pltpu

NSUB = 30


step_main = 0.1
visc_four = 0.02
diff_four = 0.02
press_scale = 0.02
step_baro = 0.1
grav_baro = 25.0
expand_temp = 0.2
contract_salt = 0.1


def laplace(quantity, wet_mask):
    centre = quantity[..., 1:-1, 1:-1]
    beside_all = (
        quantity[..., 1:-1, 2:]
        + quantity[..., 1:-1, :-2]
        + quantity[..., 2:, 1:-1]
        + quantity[..., :-2, 1:-1]
    )
    return (beside_all - 4.0 * centre) * wet_mask[..., 1:-1, 1:-1]


def diff_x(quantity):
    return 0.5 * (quantity[..., 2:-2, 3:-1] - quantity[..., 2:-2, 1:-3])


def diff_y(quantity):
    return 0.5 * (quantity[..., 3:-1, 2:-2] - quantity[..., 1:-3, 2:-2])


def tendency(padded, pressure, coriolis):
    east_vel = padded[0]
    north_vel = padded[1]
    wet_mask = padded[4]
    inner_wet = wet_mask[..., 2:-2, 2:-2]
    rotate = coriolis[:, None]
    changes = []
    for component in range(4):
        quantity = padded[component]
        advect = diff_x(east_vel * quantity) + diff_y(north_vel * quantity)
        smooth = laplace(laplace(quantity, wet_mask), wet_mask[..., 1:-1, 1:-1])
        if component == 0:
            change = rotate * north_vel[..., 2:-2, 2:-2] - diff_x(pressure) - visc_four * smooth
        elif component == 1:
            change = -rotate * east_vel[..., 2:-2, 2:-2] - diff_y(pressure) - visc_four * smooth
        else:
            change = -diff_four * smooth
        changes.append((change - advect) * inner_wet)
    return jnp.stack(changes)


def vertical_solve(provisional, mixing, wet_mask, thickness):
    levels = thickness.shape[0]
    tail_ones = (1,) * (mixing.ndim - 1)
    depth_col = thickness.reshape((levels,) + tail_ones)
    middle = (0.5 * (thickness[:-1] + thickness[1:])).reshape((levels - 1,) + tail_ones)
    coupling = mixing[:-1] * wet_mask[:-1] * wet_mask[1:] / middle
    zeros_row = jnp.zeros((1,) + mixing.shape[1:], jnp.float32)
    below_link = jnp.concatenate([coupling, zeros_row], axis=0)
    upper_link = jnp.concatenate([zeros_row, coupling], axis=0)
    diagonal = depth_col + upper_link + below_link
    source = depth_col[:, None] * provisional

    def forward(sweep, inputs):
        ratio_prev, value_prev = sweep
        upper_now, diag_now, below_now, source_now = inputs
        divisor = diag_now - upper_now * ratio_prev
        sweep_ratio = below_now / divisor
        sweep_value = (source_now + upper_now[None] * value_prev) / divisor[None]
        return ((sweep_ratio, sweep_value), (sweep_ratio, sweep_value))

    start_sweep = (
        jnp.zeros(mixing.shape[1:], jnp.float32),
        jnp.zeros(provisional.shape[1:], jnp.float32),
    )
    unused, (ratios, values) = lax.scan(
        forward, start_sweep, (upper_link, diagonal, below_link, source)
    )

    def backward(following, inputs):
        sweep_ratio, sweep_value = inputs
        result = sweep_value + sweep_ratio[None] * following
        return (result, result)

    unused_last, solved = lax.scan(
        backward, jnp.zeros(provisional.shape[1:], jnp.float32), (ratios, values), reverse=True
    )
    return solved


def zero_diff(quantity, along):
    extent = quantity.shape[along]
    ahead_part = lax.slice_in_dim(quantity, 1, extent, axis=along)
    behind = lax.slice_in_dim(quantity, 0, extent - 1, axis=along)
    zeros_row = jnp.zeros_like(lax.slice_in_dim(quantity, 0, 1, axis=along))
    return 0.5 * (
        jnp.concatenate([ahead_part, zeros_row], axis=along)
        - jnp.concatenate([zeros_row, behind], axis=along)
    )


def east_zero(quantity):
    return zero_diff(quantity, quantity.ndim - 1)


def north_zero(quantity):
    return zero_diff(quantity, quantity.ndim - 2)


def baro_step(baro_state, statics, east_diff, north_diff):
    height = baro_state[0]
    east_vel = baro_state[1]
    north_vel = baro_state[2]
    depth_ratio = statics[0]
    sea_mask = statics[1]
    rotate = statics[2]
    push_east = statics[3]
    push_north = statics[4]
    new_height = (
        height
        - step_baro * (east_diff(depth_ratio * east_vel) + north_diff(depth_ratio * north_vel))
    ) * sea_mask
    new_east = (
        east_vel + step_baro * (push_east + rotate * north_vel - grav_baro * east_diff(new_height))
    ) * sea_mask
    new_north = (
        north_vel
        + step_baro * (push_north - rotate * east_vel - grav_baro * north_diff(new_height))
    ) * sea_mask
    return jnp.stack([new_height, new_east, new_north])


def halo_3d(block, centre):
    zonal = "gx"
    merid = ("gy", "ga")
    both = ("gx", "gy", "ga")
    zonal_n = lax.axis_size(zonal)
    merid_n = lax.axis_size(merid)

    def send(piece, d_zonal, d_merid):
        if d_merid == 0:
            pairs = [(g, (g + d_zonal) % zonal_n) for g in range(zonal_n)]
            return lax.ppermute(piece, zonal, pairs)
        pairs = []
        for g in range(zonal_n):
            for m in range(merid_n):
                target = m + d_merid
                if 0 <= target < merid_n:
                    pairs.append((g * merid_n + m, ((g + d_zonal) % zonal_n) * merid_n + target))
        if d_zonal == 0:
            return lax.ppermute(piece, merid, [(s % merid_n, t % merid_n) for s, t in pairs[:merid_n - 1]])
        return lax.ppermute(piece, both, pairs)

    def masked(piece):
        wet = piece[-1:]
        return jnp.concatenate([piece[:-1] * wet, wet], axis=0)

    def take(piece, d_zonal, d_merid):
        return masked(send(piece, d_zonal, d_merid))

    w = 2
    last_rows = block[..., -w:, :]
    first_rows = block[..., :w, :]
    west = take(block[..., -w:], 1, 0)
    east = take(block[..., :w], -1, 0)
    low = take(last_rows, 0, 1)
    high = take(first_rows, 0, -1)
    low_west = take(last_rows[..., -w:], 1, 1)
    low_east = take(last_rows[..., :w], -1, 1)
    high_west = take(first_rows[..., -w:], 1, -1)
    high_east = take(first_rows[..., :w], -1, -1)
    low_band = jnp.concatenate([low_west, low, low_east], axis=-1)
    middle = jnp.concatenate([west, centre, east], axis=-1)
    high_band = jnp.concatenate([high_west, high, high_east], axis=-1)
    return jnp.concatenate([low_band, middle, high_band], axis=-2)


def shards(velocity, tracers, mixing, thickness, coriolis, land, bottom, surface, barotropic):
    levels = thickness.shape[0]
    land_f = land.astype(jnp.float32)
    level_ids = lax.broadcasted_iota(jnp.int32, (levels,) + land.shape, 0)
    wet_mask = land_f[None] * (level_ids < bottom[None]).astype(jnp.float32)
    stacked = jnp.concatenate(
        [velocity * wet_mask[None], tracers * wet_mask[None], wet_mask[None]], axis=0
    )
    raw = jnp.concatenate([velocity, tracers, wet_mask[None]], axis=0)
    padded = halo_3d(raw, stacked)
    depth_col = thickness.reshape((levels, 1, 1))
    pressure = pressure_run(thickness, padded)
    growth = tendency(padded, pressure, coriolis)
    provisional = stacked[:4] + step_main * growth
    forcing = jnp.sum(depth_col * growth[:2], axis=1)
    depth_sum = jnp.sum(depth_col * wet_mask, axis=0)
    safe_depth = jnp.maximum(depth_sum, 1.0)
    dr = depth_sum / jnp.sum(thickness)
    push_u = forcing[0] / safe_depth * land_f
    push_v = forcing[1] / safe_depth * land_f
    rotate = coriolis[:, None] * jnp.ones_like(land_f)
    fields = jnp.stack([dr, land_f, rotate, push_u, push_v, surface, barotropic[0], barotropic[1]])
    whole = gather_baro(fields)
    rows = land.shape[0]
    row_offset = jnp.full((1,), lax.axis_index(("gy", "ga")) * rows, jnp.int32)
    mine = baro_run(whole, row_offset, land.shape[1])
    average = mine[3:]
    solved = solve_columns(provisional, mixing, wet_mask, thickness)
    thick_col = thickness.reshape((levels, 1, 1))
    depth_mean = jnp.sum(thick_col[None] * wet_mask[None] * solved[:2], axis=1) / safe_depth
    new_velocity = (solved[:2] - depth_mean[:, None] + average[:, None]) * wet_mask[None]
    new_tracers = solved[2:]
    return (new_velocity, new_tracers, mine[0], mine[1:3])


BARO_HALO = 64


def gather_baro(fields):
    count = lax.axis_size("gx")
    forward = [(i, (i + 1) % count) for i in range(count)]
    backward = [(target, source) for source, target in forward]
    low = lax.ppermute(fields[..., -BARO_HALO:], "gx", forward)
    high = lax.ppermute(fields[..., :BARO_HALO], "gx", backward)
    wide = jnp.concatenate([low, fields, high], axis=-1)
    merid = ("gy", "ga")
    parts = lax.axis_size(merid)
    blocks = [wide]
    for shift in range(1, parts):
        pairs = [(d, (d - shift) % parts) for d in range(parts)]
        blocks.append(lax.ppermute(wide, merid, pairs))
    return jnp.stack(blocks)


def baro_kernel(off_ref, f_ref, o_ref):
    parts = f_ref.shape[0]
    block_rows = f_ref.shape[2]
    rows = parts * block_rows
    cols = f_ref.shape[3]

    def field(index):
        return jnp.concatenate([f_ref[part, index] for part in range(parts)], axis=0)

    depth_ratio = field(0)
    sea_mask = field(1)
    rotate = field(2)
    push_east = field(3)
    push_north = field(4)
    offset = off_ref[0]
    last_local = rows - 1 - offset
    first_local = jnp.where(offset == 0, 0, rows - offset)
    row = lax.broadcasted_iota(jnp.int32, (rows, cols), 0)
    not_last = row != last_local
    not_first = row != first_local

    def east_diff(q):
        return 0.5 * (pltpu.roll(q, cols - 1, 1) - pltpu.roll(q, 1, 1))

    def north_diff(q):
        ahead = jnp.where(not_last, pltpu.roll(q, rows - 1, 0), 0.0)
        behind = jnp.where(not_first, pltpu.roll(q, 1, 0), 0.0)
        return 0.5 * (ahead - behind)

    def body(turn, carry):
        height, east_vel, north_vel, sum_east, sum_north = carry
        height = (
            height
            - step_baro * (east_diff(depth_ratio * east_vel) + north_diff(depth_ratio * north_vel))
        ) * sea_mask
        new_east = (
            east_vel + step_baro * (push_east + rotate * north_vel - grav_baro * east_diff(height))
        ) * sea_mask
        new_north = (
            north_vel
            + step_baro * (push_north - rotate * east_vel - grav_baro * north_diff(height))
        ) * sea_mask
        return (height, new_east, new_north, sum_east + new_east, sum_north + new_north)

    zeros = jnp.zeros((rows, cols), jnp.float32)
    carry = (field(5), field(6), field(7), zeros, zeros)
    height, east_vel, north_vel, sum_east, sum_north = lax.fori_loop(0, NSUB, body, carry)
    finals = (height, east_vel, north_vel, sum_east / NSUB, sum_north / NSUB)
    out_cols = o_ref.shape[2]
    for index in range(5):
        o_ref[index] = pltpu.roll(finals[index][:block_rows], cols - BARO_HALO, 1)[:, :out_cols]


def baro_run(whole, row_offset, out_cols):
    return pl.pallas_call(
        baro_kernel,
        out_shape=jax.ShapeDtypeStruct((5, whole.shape[2], out_cols), jnp.float32),
        in_specs=[pl.BlockSpec(memory_space=pltpu.SMEM), pl.BlockSpec(memory_space=pltpu.VMEM)],
        out_specs=pl.BlockSpec(memory_space=pltpu.VMEM),
    )(row_offset, whole)


def pressure_kernel(th_ref, pad_ref, o_ref):
    levels = pad_ref.shape[1]

    def body(k, overlying):
        weight = (contract_salt * pad_ref[3, k] - expand_temp * pad_ref[2, k]) * pad_ref[4, k] * th_ref[k]
        o_ref[k] = press_scale * (overlying + 0.5 * weight)
        return overlying + weight

    lax.fori_loop(0, levels, body, jnp.zeros(pad_ref.shape[2:], jnp.float32))


def pressure_run(thickness, padded):
    return pl.pallas_call(
        pressure_kernel,
        out_shape=jax.ShapeDtypeStruct(padded.shape[1:], jnp.float32),
        in_specs=[pl.BlockSpec(memory_space=pltpu.SMEM), pl.BlockSpec(memory_space=pltpu.VMEM)],
        out_specs=pl.BlockSpec(memory_space=pltpu.VMEM),
    )(thickness, padded)


def solve_kernel(th_ref, prov_ref, mix_ref, wet_ref, o_ref, ratio_ref):
    levels = mix_ref.shape[0]
    shape = mix_ref.shape[1:]
    comps = prov_ref.shape[0]

    def below_of(k):
        nxt = jnp.minimum(k + 1, levels - 1)
        middle = 0.5 * (th_ref[k] + th_ref[nxt])
        coupling = mix_ref[k] * wet_ref[k] * wet_ref[nxt] / middle
        return jnp.where(k < levels - 1, coupling, 0.0)

    def forward(k, carry):
        upper, ratio_prev, value_prev = carry
        below = below_of(k)
        depth = th_ref[k]
        diagonal = depth + upper + below
        divisor = diagonal - upper * ratio_prev
        ratio = below / divisor
        ratio_ref[k] = ratio
        values = []
        for c in range(comps):
            value = (depth * prov_ref[c, k] + upper * value_prev[c]) / divisor
            o_ref[c, k] = value
            values.append(value)
        return (below, ratio, tuple(values))

    zeros = jnp.zeros(shape, jnp.float32)
    lax.fori_loop(0, levels, forward, (zeros, zeros, (zeros,) * comps))

    def backward(step, following):
        k = levels - 1 - step
        ratio = ratio_ref[k]
        results = []
        for c in range(comps):
            result = o_ref[c, k] + ratio * following[c]
            o_ref[c, k] = result
            results.append(result)
        return tuple(results)

    lax.fori_loop(0, levels, backward, (zeros,) * comps)


def solve_columns(provisional, mixing, wet_mask, thickness):
    return pl.pallas_call(
        solve_kernel,
        out_shape=jax.ShapeDtypeStruct(provisional.shape, jnp.float32),
        in_specs=[pl.BlockSpec(memory_space=pltpu.SMEM)]
        + [pl.BlockSpec(memory_space=pltpu.VMEM)] * 3,
        out_specs=pl.BlockSpec(memory_space=pltpu.VMEM),
        scratch_shapes=[pltpu.VMEM(mixing.shape, jnp.float32)],
    )(thickness, provisional, mixing, wet_mask)


def solution(mesh):
    return jax.shard_map(
        shards,
        mesh=mesh,
        in_specs=(
            P(None, None, ("gy", "ga"), "gx"),
            P(None, None, ("gy", "ga"), "gx"),
            P(None, ("gy", "ga"), "gx"),
            P(),
            P(("gy", "ga")),
            P(("gy", "ga"), "gx"),
            P(("gy", "ga"), "gx"),
            P(("gy", "ga"), "gx"),
            P(None, ("gy", "ga"), "gx"),
        ),
        out_specs=(
            P(None, None, ("gy", "ga"), "gx"),
            P(None, None, ("gy", "ga"), "gx"),
            P(("gy", "ga"), "gx"),
            P(None, ("gy", "ga"), "gx"),
        ),
        check_vma=False,
    )
```

```python
import jax
import jax.numpy as jnp
from jax import lax
from jax.sharding import PartitionSpec as P
from jax.experimental import pallas as pl
from jax.experimental.pallas import tpu as pltpu

NSUB = 30


step_main = 0.1
visc_four = 0.02
diff_four = 0.02
press_scale = 0.02
step_baro = 0.1
grav_baro = 25.0
expand_temp = 0.2
contract_salt = 0.1


def laplace(quantity, wet_mask):
    centre = quantity[..., 1:-1, 1:-1]
    beside_all = (
        quantity[..., 1:-1, 2:]
        + quantity[..., 1:-1, :-2]
        + quantity[..., 2:, 1:-1]
        + quantity[..., :-2, 1:-1]
    )
    return (beside_all - 4.0 * centre) * wet_mask[..., 1:-1, 1:-1]


def diff_x(quantity):
    return 0.5 * (quantity[..., 2:-2, 3:-1] - quantity[..., 2:-2, 1:-3])


def diff_y(quantity):
    return 0.5 * (quantity[..., 3:-1, 2:-2] - quantity[..., 1:-3, 2:-2])


def tendency(padded, pressure, coriolis):
    east_vel = padded[0]
    north_vel = padded[1]
    wet_mask = padded[4]
    inner_wet = wet_mask[..., 2:-2, 2:-2]
    rotate = coriolis[:, None]
    changes = []
    for component in range(4):
        quantity = padded[component]
        advect = diff_x(east_vel * quantity) + diff_y(north_vel * quantity)
        smooth = laplace(laplace(quantity, wet_mask), wet_mask[..., 1:-1, 1:-1])
        if component == 0:
            change = rotate * north_vel[..., 2:-2, 2:-2] - diff_x(pressure) - visc_four * smooth
        elif component == 1:
            change = -rotate * east_vel[..., 2:-2, 2:-2] - diff_y(pressure) - visc_four * smooth
        else:
            change = -diff_four * smooth
        changes.append((change - advect) * inner_wet)
    return jnp.stack(changes)


def vertical_solve(provisional, mixing, wet_mask, thickness):
    levels = thickness.shape[0]
    tail_ones = (1,) * (mixing.ndim - 1)
    depth_col = thickness.reshape((levels,) + tail_ones)
    middle = (0.5 * (thickness[:-1] + thickness[1:])).reshape((levels - 1,) + tail_ones)
    coupling = mixing[:-1] * wet_mask[:-1] * wet_mask[1:] / middle
    zeros_row = jnp.zeros((1,) + mixing.shape[1:], jnp.float32)
    below_link = jnp.concatenate([coupling, zeros_row], axis=0)
    upper_link = jnp.concatenate([zeros_row, coupling], axis=0)
    diagonal = depth_col + upper_link + below_link
    source = depth_col[:, None] * provisional

    def forward(sweep, inputs):
        ratio_prev, value_prev = sweep
        upper_now, diag_now, below_now, source_now = inputs
        divisor = diag_now - upper_now * ratio_prev
        sweep_ratio = below_now / divisor
        sweep_value = (source_now + upper_now[None] * value_prev) / divisor[None]
        return ((sweep_ratio, sweep_value), (sweep_ratio, sweep_value))

    start_sweep = (
        jnp.zeros(mixing.shape[1:], jnp.float32),
        jnp.zeros(provisional.shape[1:], jnp.float32),
    )
    unused, (ratios, values) = lax.scan(
        forward, start_sweep, (upper_link, diagonal, below_link, source)
    )

    def backward(following, inputs):
        sweep_ratio, sweep_value = inputs
        result = sweep_value + sweep_ratio[None] * following
        return (result, result)

    unused_last, solved = lax.scan(
        backward, jnp.zeros(provisional.shape[1:], jnp.float32), (ratios, values), reverse=True
    )
    return solved


def zero_diff(quantity, along):
    extent = quantity.shape[along]
    ahead_part = lax.slice_in_dim(quantity, 1, extent, axis=along)
    behind = lax.slice_in_dim(quantity, 0, extent - 1, axis=along)
    zeros_row = jnp.zeros_like(lax.slice_in_dim(quantity, 0, 1, axis=along))
    return 0.5 * (
        jnp.concatenate([ahead_part, zeros_row], axis=along)
        - jnp.concatenate([zeros_row, behind], axis=along)
    )


def east_zero(quantity):
    return zero_diff(quantity, quantity.ndim - 1)


def north_zero(quantity):
    return zero_diff(quantity, quantity.ndim - 2)


def baro_step(baro_state, statics, east_diff, north_diff):
    height = baro_state[0]
    east_vel = baro_state[1]
    north_vel = baro_state[2]
    depth_ratio = statics[0]
    sea_mask = statics[1]
    rotate = statics[2]
    push_east = statics[3]
    push_north = statics[4]
    new_height = (
        height
        - step_baro * (east_diff(depth_ratio * east_vel) + north_diff(depth_ratio * north_vel))
    ) * sea_mask
    new_east = (
        east_vel + step_baro * (push_east + rotate * north_vel - grav_baro * east_diff(new_height))
    ) * sea_mask
    new_north = (
        north_vel
        + step_baro * (push_north - rotate * east_vel - grav_baro * north_diff(new_height))
    ) * sea_mask
    return jnp.stack([new_height, new_east, new_north])


def halo_3d(block):
    zonal = "gx"
    merid = ("gy", "ga")
    both = ("gx", "gy", "ga")
    zonal_n = lax.axis_size(zonal)
    merid_n = lax.axis_size(merid)

    def send(piece, d_zonal, d_merid):
        if d_merid == 0:
            pairs = [(g, (g + d_zonal) % zonal_n) for g in range(zonal_n)]
            return lax.ppermute(piece, zonal, pairs)
        pairs = []
        for g in range(zonal_n):
            for m in range(merid_n):
                target = m + d_merid
                if 0 <= target < merid_n:
                    pairs.append((g * merid_n + m, ((g + d_zonal) % zonal_n) * merid_n + target))
        if d_zonal == 0:
            return lax.ppermute(piece, merid, [(s % merid_n, t % merid_n) for s, t in pairs[:merid_n - 1]])
        return lax.ppermute(piece, both, pairs)

    w = 2
    last_rows = block[..., -w:, :]
    first_rows = block[..., :w, :]
    west = send(block[..., -w:], 1, 0)
    east = send(block[..., :w], -1, 0)
    low = send(last_rows, 0, 1)
    high = send(first_rows, 0, -1)
    low_west = send(last_rows[..., -w:], 1, 1)
    low_east = send(last_rows[..., :w], -1, 1)
    high_west = send(first_rows[..., -w:], 1, -1)
    high_east = send(first_rows[..., :w], -1, -1)
    low_band = jnp.concatenate([low_west, low, low_east], axis=-1)
    middle = jnp.concatenate([west, block, east], axis=-1)
    high_band = jnp.concatenate([high_west, high, high_east], axis=-1)
    return jnp.concatenate([low_band, middle, high_band], axis=-2)


def shards(velocity, tracers, mixing, thickness, coriolis, land, bottom, surface, barotropic):
    levels = thickness.shape[0]
    land_f = land.astype(jnp.float32)
    level_ids = lax.broadcasted_iota(jnp.int32, (levels,) + land.shape, 0)
    wet_mask = land_f[None] * (level_ids < bottom[None]).astype(jnp.float32)
    stacked = jnp.concatenate(
        [velocity * wet_mask[None], tracers * wet_mask[None], wet_mask[None]], axis=0
    )
    padded = halo_3d(stacked)
    depth_col = thickness.reshape((levels, 1, 1))
    pressure = pressure_run(thickness, padded)
    growth = tendency(padded, pressure, coriolis)
    provisional = stacked[:4] + step_main * growth
    forcing = jnp.sum(depth_col * growth[:2], axis=1)
    depth_sum = jnp.sum(depth_col * wet_mask, axis=0)
    safe_depth = jnp.maximum(depth_sum, 1.0)
    dr = depth_sum / jnp.sum(thickness)
    push_u = forcing[0] / safe_depth * land_f
    push_v = forcing[1] / safe_depth * land_f
    rotate = coriolis[:, None] * jnp.ones_like(land_f)
    fields = jnp.stack([dr, land_f, rotate, push_u, push_v, surface, barotropic[0], barotropic[1]])
    whole = gather_baro(fields)
    rows = land.shape[0]
    row_offset = jnp.full((1,), lax.axis_index(("gy", "ga")) * rows, jnp.int32)
    mine = baro_run(whole, row_offset, land.shape[1])
    average = mine[3:]
    solved = solve_columns(provisional, mixing, wet_mask, thickness)
    thick_col = thickness.reshape((levels, 1, 1))
    depth_mean = jnp.sum(thick_col[None] * wet_mask[None] * solved[:2], axis=1) / safe_depth
    new_velocity = (solved[:2] - depth_mean[:, None] + average[:, None]) * wet_mask[None]
    new_tracers = solved[2:]
    return (new_velocity, new_tracers, mine[0], mine[1:3])


BARO_HALO = 64


def gather_baro(fields):
    count = lax.axis_size("gx")
    forward = [(i, (i + 1) % count) for i in range(count)]
    backward = [(target, source) for source, target in forward]
    low = lax.ppermute(fields[..., -BARO_HALO:], "gx", forward)
    high = lax.ppermute(fields[..., :BARO_HALO], "gx", backward)
    wide = jnp.concatenate([low, fields, high], axis=-1)
    merid = ("gy", "ga")
    parts = lax.axis_size(merid)
    blocks = [wide]
    for shift in range(1, parts):
        pairs = [(d, (d - shift) % parts) for d in range(parts)]
        blocks.append(lax.ppermute(wide, merid, pairs))
    return jnp.stack(blocks)


def baro_kernel(off_ref, f_ref, o_ref):
    parts = f_ref.shape[0]
    block_rows = f_ref.shape[2]
    rows = parts * block_rows
    cols = f_ref.shape[3]

    def field(index):
        return jnp.concatenate([f_ref[part, index] for part in range(parts)], axis=0)

    depth_ratio = field(0)
    sea_mask = field(1)
    rotate = field(2)
    push_east = field(3)
    push_north = field(4)
    offset = off_ref[0]
    last_local = rows - 1 - offset
    first_local = jnp.where(offset == 0, 0, rows - offset)
    row = lax.broadcasted_iota(jnp.int32, (rows, cols), 0)
    not_last = row != last_local
    not_first = row != first_local

    def east_diff(q):
        return 0.5 * (pltpu.roll(q, cols - 1, 1) - pltpu.roll(q, 1, 1))

    def north_diff(q):
        ahead = jnp.where(not_last, pltpu.roll(q, rows - 1, 0), 0.0)
        behind = jnp.where(not_first, pltpu.roll(q, 1, 0), 0.0)
        return 0.5 * (ahead - behind)

    def body(turn, carry):
        height, east_vel, north_vel, sum_east, sum_north = carry
        height = (
            height
            - step_baro * (east_diff(depth_ratio * east_vel) + north_diff(depth_ratio * north_vel))
        ) * sea_mask
        new_east = (
            east_vel + step_baro * (push_east + rotate * north_vel - grav_baro * east_diff(height))
        ) * sea_mask
        new_north = (
            north_vel
            + step_baro * (push_north - rotate * east_vel - grav_baro * north_diff(height))
        ) * sea_mask
        return (height, new_east, new_north, sum_east + new_east, sum_north + new_north)

    zeros = jnp.zeros((rows, cols), jnp.float32)
    carry = (field(5), field(6), field(7), zeros, zeros)
    height, east_vel, north_vel, sum_east, sum_north = lax.fori_loop(0, NSUB, body, carry)
    finals = (height, east_vel, north_vel, sum_east / NSUB, sum_north / NSUB)
    out_cols = o_ref.shape[2]
    for index in range(5):
        o_ref[index] = pltpu.roll(finals[index][:block_rows], cols - BARO_HALO, 1)[:, :out_cols]


def baro_run(whole, row_offset, out_cols):
    return pl.pallas_call(
        baro_kernel,
        out_shape=jax.ShapeDtypeStruct((5, whole.shape[2], out_cols), jnp.float32),
        in_specs=[pl.BlockSpec(memory_space=pltpu.SMEM), pl.BlockSpec(memory_space=pltpu.VMEM)],
        out_specs=pl.BlockSpec(memory_space=pltpu.VMEM),
    )(row_offset, whole)


def pressure_kernel(th_ref, pad_ref, o_ref):
    levels = pad_ref.shape[1]

    def body(k, overlying):
        weight = (contract_salt * pad_ref[3, k] - expand_temp * pad_ref[2, k]) * pad_ref[4, k] * th_ref[k]
        o_ref[k] = press_scale * (overlying + 0.5 * weight)
        return overlying + weight

    lax.fori_loop(0, levels, body, jnp.zeros(pad_ref.shape[2:], jnp.float32), unroll=8)


def pressure_run(thickness, padded):
    return pl.pallas_call(
        pressure_kernel,
        out_shape=jax.ShapeDtypeStruct(padded.shape[1:], jnp.float32),
        in_specs=[pl.BlockSpec(memory_space=pltpu.SMEM), pl.BlockSpec(memory_space=pltpu.VMEM)],
        out_specs=pl.BlockSpec(memory_space=pltpu.VMEM),
    )(thickness, padded)


def solve_kernel(th_ref, prov_ref, mix_ref, wet_ref, o_ref, ratio_ref):
    levels = mix_ref.shape[0]
    shape = mix_ref.shape[1:]
    comps = prov_ref.shape[0]

    def below_of(k):
        nxt = jnp.minimum(k + 1, levels - 1)
        middle = 0.5 * (th_ref[k] + th_ref[nxt])
        coupling = mix_ref[k] * wet_ref[k] * wet_ref[nxt] / middle
        return jnp.where(k < levels - 1, coupling, 0.0)

    def forward(k, carry):
        upper, ratio_prev, value_prev = carry
        below = below_of(k)
        depth = th_ref[k]
        diagonal = depth + upper + below
        divisor = diagonal - upper * ratio_prev
        inverse = 1.0 / divisor
        ratio = below * inverse
        ratio_ref[k] = ratio
        values = []
        for c in range(comps):
            value = (depth * prov_ref[c, k] + upper * value_prev[c]) * inverse
            o_ref[c, k] = value
            values.append(value)
        return (below, ratio, tuple(values))

    zeros = jnp.zeros(shape, jnp.float32)
    lax.fori_loop(0, levels, forward, (zeros, zeros, (zeros,) * comps), unroll=4)

    def backward(step, following):
        k = levels - 1 - step
        ratio = ratio_ref[k]
        results = []
        for c in range(comps):
            result = o_ref[c, k] + ratio * following[c]
            o_ref[c, k] = result
            results.append(result)
        return tuple(results)

    lax.fori_loop(0, levels, backward, (zeros,) * comps, unroll=4)


def solve_columns(provisional, mixing, wet_mask, thickness):
    return pl.pallas_call(
        solve_kernel,
        out_shape=jax.ShapeDtypeStruct(provisional.shape, jnp.float32),
        in_specs=[pl.BlockSpec(memory_space=pltpu.SMEM)]
        + [pl.BlockSpec(memory_space=pltpu.VMEM)] * 3,
        out_specs=pl.BlockSpec(memory_space=pltpu.VMEM),
        scratch_shapes=[pltpu.VMEM(mixing.shape, jnp.float32)],
    )(thickness, provisional, mixing, wet_mask)


def solution(mesh):
    return jax.shard_map(
        shards,
        mesh=mesh,
        in_specs=(
            P(None, None, ("gy", "ga"), "gx"),
            P(None, None, ("gy", "ga"), "gx"),
            P(None, ("gy", "ga"), "gx"),
            P(),
            P(("gy", "ga")),
            P(("gy", "ga"), "gx"),
            P(("gy", "ga"), "gx"),
            P(("gy", "ga"), "gx"),
            P(None, ("gy", "ga"), "gx"),
        ),
        out_specs=(
            P(None, None, ("gy", "ga"), "gx"),
            P(None, None, ("gy", "ga"), "gx"),
            P(("gy", "ga"), "gx"),
            P(None, ("gy", "ga"), "gx"),
        ),
        check_vma=False,
    )
```

```python
import jax
import jax.numpy as jnp
from jax import lax
from jax.sharding import PartitionSpec as P
from jax.experimental import pallas as pl
from jax.experimental.pallas import tpu as pltpu

NSUB = 30


step_main = 0.1
visc_four = 0.02
diff_four = 0.02
press_scale = 0.02
step_baro = 0.1
grav_baro = 25.0
expand_temp = 0.2
contract_salt = 0.1


def laplace(quantity, wet_mask):
    centre = quantity[..., 1:-1, 1:-1]
    beside_all = (
        quantity[..., 1:-1, 2:]
        + quantity[..., 1:-1, :-2]
        + quantity[..., 2:, 1:-1]
        + quantity[..., :-2, 1:-1]
    )
    return (beside_all - 4.0 * centre) * wet_mask[..., 1:-1, 1:-1]


def diff_x(quantity):
    return 0.5 * (quantity[..., 2:-2, 3:-1] - quantity[..., 2:-2, 1:-3])


def diff_y(quantity):
    return 0.5 * (quantity[..., 3:-1, 2:-2] - quantity[..., 1:-3, 2:-2])


def tendency(padded, pressure, coriolis):
    east_vel = padded[0]
    north_vel = padded[1]
    wet_mask = padded[4]
    inner_wet = wet_mask[..., 2:-2, 2:-2]
    rotate = coriolis[:, None]
    changes = []
    for component in range(4):
        quantity = padded[component]
        advect = diff_x(east_vel * quantity) + diff_y(north_vel * quantity)
        smooth = laplace(laplace(quantity, wet_mask), wet_mask[..., 1:-1, 1:-1])
        if component == 0:
            change = rotate * north_vel[..., 2:-2, 2:-2] - diff_x(pressure) - visc_four * smooth
        elif component == 1:
            change = -rotate * east_vel[..., 2:-2, 2:-2] - diff_y(pressure) - visc_four * smooth
        else:
            change = -diff_four * smooth
        changes.append((change - advect) * inner_wet)
    return jnp.stack(changes)


def vertical_solve(provisional, mixing, wet_mask, thickness):
    levels = thickness.shape[0]
    tail_ones = (1,) * (mixing.ndim - 1)
    depth_col = thickness.reshape((levels,) + tail_ones)
    middle = (0.5 * (thickness[:-1] + thickness[1:])).reshape((levels - 1,) + tail_ones)
    coupling = mixing[:-1] * wet_mask[:-1] * wet_mask[1:] / middle
    zeros_row = jnp.zeros((1,) + mixing.shape[1:], jnp.float32)
    below_link = jnp.concatenate([coupling, zeros_row], axis=0)
    upper_link = jnp.concatenate([zeros_row, coupling], axis=0)
    diagonal = depth_col + upper_link + below_link
    source = depth_col[:, None] * provisional

    def forward(sweep, inputs):
        ratio_prev, value_prev = sweep
        upper_now, diag_now, below_now, source_now = inputs
        divisor = diag_now - upper_now * ratio_prev
        sweep_ratio = below_now / divisor
        sweep_value = (source_now + upper_now[None] * value_prev) / divisor[None]
        return ((sweep_ratio, sweep_value), (sweep_ratio, sweep_value))

    start_sweep = (
        jnp.zeros(mixing.shape[1:], jnp.float32),
        jnp.zeros(provisional.shape[1:], jnp.float32),
    )
    unused, (ratios, values) = lax.scan(
        forward, start_sweep, (upper_link, diagonal, below_link, source)
    )

    def backward(following, inputs):
        sweep_ratio, sweep_value = inputs
        result = sweep_value + sweep_ratio[None] * following
        return (result, result)

    unused_last, solved = lax.scan(
        backward, jnp.zeros(provisional.shape[1:], jnp.float32), (ratios, values), reverse=True
    )
    return solved


def zero_diff(quantity, along):
    extent = quantity.shape[along]
    ahead_part = lax.slice_in_dim(quantity, 1, extent, axis=along)
    behind = lax.slice_in_dim(quantity, 0, extent - 1, axis=along)
    zeros_row = jnp.zeros_like(lax.slice_in_dim(quantity, 0, 1, axis=along))
    return 0.5 * (
        jnp.concatenate([ahead_part, zeros_row], axis=along)
        - jnp.concatenate([zeros_row, behind], axis=along)
    )


def east_zero(quantity):
    return zero_diff(quantity, quantity.ndim - 1)


def north_zero(quantity):
    return zero_diff(quantity, quantity.ndim - 2)


def baro_step(baro_state, statics, east_diff, north_diff):
    height = baro_state[0]
    east_vel = baro_state[1]
    north_vel = baro_state[2]
    depth_ratio = statics[0]
    sea_mask = statics[1]
    rotate = statics[2]
    push_east = statics[3]
    push_north = statics[4]
    new_height = (
        height
        - step_baro * (east_diff(depth_ratio * east_vel) + north_diff(depth_ratio * north_vel))
    ) * sea_mask
    new_east = (
        east_vel + step_baro * (push_east + rotate * north_vel - grav_baro * east_diff(new_height))
    ) * sea_mask
    new_north = (
        north_vel
        + step_baro * (push_north - rotate * east_vel - grav_baro * north_diff(new_height))
    ) * sea_mask
    return jnp.stack([new_height, new_east, new_north])


def halo_3d(block):
    zonal = "gx"
    merid = ("gy", "ga")
    both = ("gx", "gy", "ga")
    zonal_n = lax.axis_size(zonal)
    merid_n = lax.axis_size(merid)

    def send(piece, d_zonal, d_merid):
        if d_merid == 0:
            pairs = [(g, (g + d_zonal) % zonal_n) for g in range(zonal_n)]
            return lax.ppermute(piece, zonal, pairs)
        pairs = []
        for g in range(zonal_n):
            for m in range(merid_n):
                target = m + d_merid
                if 0 <= target < merid_n:
                    pairs.append((g * merid_n + m, ((g + d_zonal) % zonal_n) * merid_n + target))
        if d_zonal == 0:
            return lax.ppermute(piece, merid, [(s % merid_n, t % merid_n) for s, t in pairs[:merid_n - 1]])
        return lax.ppermute(piece, both, pairs)

    w = 2
    last_rows = block[..., -w:, :]
    first_rows = block[..., :w, :]
    west = send(block[..., -w:], 1, 0)
    east = send(block[..., :w], -1, 0)
    low = send(last_rows, 0, 1)
    high = send(first_rows, 0, -1)
    low_west = send(last_rows[..., -w:], 1, 1)
    low_east = send(last_rows[..., :w], -1, 1)
    high_west = send(first_rows[..., -w:], 1, -1)
    high_east = send(first_rows[..., :w], -1, -1)
    low_band = jnp.concatenate([low_west, low, low_east], axis=-1)
    middle = jnp.concatenate([west, block, east], axis=-1)
    high_band = jnp.concatenate([high_west, high, high_east], axis=-1)
    return jnp.concatenate([low_band, middle, high_band], axis=-2)


def shards(velocity, tracers, mixing, thickness, coriolis, land, bottom, surface, barotropic):
    levels = thickness.shape[0]
    land_f = land.astype(jnp.float32)
    level_ids = lax.broadcasted_iota(jnp.int32, (levels,) + land.shape, 0)
    wet_mask = land_f[None] * (level_ids < bottom[None]).astype(jnp.float32)
    stacked = jnp.concatenate(
        [velocity * wet_mask[None], tracers * wet_mask[None], wet_mask[None]], axis=0
    )
    padded = halo_3d(stacked)
    depth_col = thickness.reshape((levels, 1, 1))
    pressure = pressure_run(thickness, padded)
    growth = tendency(padded, pressure, coriolis)
    provisional = stacked[:4] + step_main * growth
    forcing = jnp.sum(depth_col * growth[:2], axis=1)
    depth_sum = jnp.sum(depth_col * wet_mask, axis=0)
    safe_depth = jnp.maximum(depth_sum, 1.0)
    dr = depth_sum / jnp.sum(thickness)
    push_u = forcing[0] / safe_depth * land_f
    push_v = forcing[1] / safe_depth * land_f
    rotate = coriolis[:, None] * jnp.ones_like(land_f)
    fields = jnp.stack([dr, land_f, rotate, push_u, push_v, surface, barotropic[0], barotropic[1]])
    whole = gather_baro(fields)
    rows = land.shape[0]
    row_offset = jnp.full((1,), lax.axis_index(("gy", "ga")) * rows, jnp.int32)
    solved_uv, new_tracers = solve_columns(provisional, mixing, wet_mask, thickness)
    thick_col = thickness.reshape((levels, 1, 1))
    depth_mean = jnp.sum(thick_col[None] * wet_mask[None] * solved_uv, axis=1) / safe_depth
    new_velocity, mine = baro_run(whole, row_offset, solved_uv, depth_mean, wet_mask)
    return (new_velocity, new_tracers, mine[0], mine[1:3])


BARO_HALO = 64


def gather_baro(fields):
    count = lax.axis_size("gx")
    forward = [(i, (i + 1) % count) for i in range(count)]
    backward = [(target, source) for source, target in forward]
    low = lax.ppermute(fields[..., -BARO_HALO:], "gx", forward)
    high = lax.ppermute(fields[..., :BARO_HALO], "gx", backward)
    wide = jnp.concatenate([low, fields, high], axis=-1)
    merid = ("gy", "ga")
    parts = lax.axis_size(merid)
    blocks = [wide]
    for shift in range(1, parts):
        pairs = [(d, (d - shift) % parts) for d in range(parts)]
        blocks.append(lax.ppermute(wide, merid, pairs))
    return jnp.stack(blocks)


def baro_kernel(off_ref, f_ref, uv_ref, dm_ref, wet_ref, nv_ref, o_ref):
    parts = f_ref.shape[0]
    block_rows = f_ref.shape[2]
    rows = parts * block_rows
    cols = f_ref.shape[3]

    def field(index):
        return jnp.concatenate([f_ref[part, index] for part in range(parts)], axis=0)

    depth_ratio = field(0)
    sea_mask = field(1)
    rotate = field(2)
    push_east = field(3)
    push_north = field(4)
    offset = off_ref[0]
    last_local = rows - 1 - offset
    first_local = jnp.where(offset == 0, 0, rows - offset)
    row = lax.broadcasted_iota(jnp.int32, (rows, cols), 0)
    not_last = row != last_local
    not_first = row != first_local

    def east_diff(q):
        return 0.5 * (pltpu.roll(q, cols - 1, 1) - pltpu.roll(q, 1, 1))

    def north_diff(q):
        ahead = jnp.where(not_last, pltpu.roll(q, rows - 1, 0), 0.0)
        behind = jnp.where(not_first, pltpu.roll(q, 1, 0), 0.0)
        return 0.5 * (ahead - behind)

    def body(turn, carry):
        height, east_vel, north_vel, sum_east, sum_north = carry
        height = (
            height
            - step_baro * (east_diff(depth_ratio * east_vel) + north_diff(depth_ratio * north_vel))
        ) * sea_mask
        new_east = (
            east_vel + step_baro * (push_east + rotate * north_vel - grav_baro * east_diff(height))
        ) * sea_mask
        new_north = (
            north_vel
            + step_baro * (push_north - rotate * east_vel - grav_baro * north_diff(height))
        ) * sea_mask
        return (height, new_east, new_north, sum_east + new_east, sum_north + new_north)

    zeros = jnp.zeros((rows, cols), jnp.float32)
    carry = (field(5), field(6), field(7), zeros, zeros)
    height, east_vel, north_vel, sum_east, sum_north = lax.fori_loop(0, NSUB, body, carry)
    finals = (height, east_vel, north_vel, sum_east / NSUB, sum_north / NSUB)
    out_cols = o_ref.shape[2]
    mine = [
        pltpu.roll(finals[index][:block_rows], cols - BARO_HALO, 1)[:, :out_cols] for index in range(5)
    ]
    for index in range(3):
        o_ref[index] = mine[index]
    mean_east = dm_ref[0]
    mean_north = dm_ref[1]

    def level(k, carry):
        wet = wet_ref[k]
        nv_ref[0, k] = (uv_ref[0, k] - mean_east + mine[3]) * wet
        nv_ref[1, k] = (uv_ref[1, k] - mean_north + mine[4]) * wet
        return carry

    lax.fori_loop(0, wet_ref.shape[0], level, 0, unroll=4)


def baro_run(whole, row_offset, solved_uv, depth_mean, wet_mask):
    vmem = pl.BlockSpec(memory_space=pltpu.VMEM)
    return pl.pallas_call(
        baro_kernel,
        out_shape=[
            jax.ShapeDtypeStruct(solved_uv.shape, jnp.float32),
            jax.ShapeDtypeStruct((3,) + wet_mask.shape[1:], jnp.float32),
        ],
        in_specs=[pl.BlockSpec(memory_space=pltpu.SMEM)] + [vmem] * 4,
        out_specs=[vmem, vmem],
    )(row_offset, whole, solved_uv, depth_mean, wet_mask)


def pressure_kernel(th_ref, pad_ref, o_ref):
    levels = pad_ref.shape[1]

    def body(k, overlying):
        weight = (contract_salt * pad_ref[3, k] - expand_temp * pad_ref[2, k]) * pad_ref[4, k] * th_ref[k]
        o_ref[k] = press_scale * (overlying + 0.5 * weight)
        return overlying + weight

    lax.fori_loop(0, levels, body, jnp.zeros(pad_ref.shape[2:], jnp.float32), unroll=8)


def pressure_run(thickness, padded):
    return pl.pallas_call(
        pressure_kernel,
        out_shape=jax.ShapeDtypeStruct(padded.shape[1:], jnp.float32),
        in_specs=[pl.BlockSpec(memory_space=pltpu.SMEM), pl.BlockSpec(memory_space=pltpu.VMEM)],
        out_specs=pl.BlockSpec(memory_space=pltpu.VMEM),
    )(thickness, padded)


def solve_kernel(th_ref, prov_ref, mix_ref, wet_ref, uv_ref, ts_ref, ratio_ref):
    levels = mix_ref.shape[0]
    shape = mix_ref.shape[1:]
    comps = prov_ref.shape[0]
    outs = [uv_ref.at[0], uv_ref.at[1], ts_ref.at[0], ts_ref.at[1]]

    def below_of(k):
        nxt = jnp.minimum(k + 1, levels - 1)
        middle = 0.5 * (th_ref[k] + th_ref[nxt])
        coupling = mix_ref[k] * wet_ref[k] * wet_ref[nxt] / middle
        return jnp.where(k < levels - 1, coupling, 0.0)

    def forward(k, carry):
        upper, ratio_prev, value_prev = carry
        below = below_of(k)
        depth = th_ref[k]
        diagonal = depth + upper + below
        divisor = diagonal - upper * ratio_prev
        inverse = 1.0 / divisor
        ratio = below * inverse
        ratio_ref[k] = ratio
        values = []
        for c in range(comps):
            value = (depth * prov_ref[c, k] + upper * value_prev[c]) * inverse
            outs[c][k] = value
            values.append(value)
        return (below, ratio, tuple(values))

    zeros = jnp.zeros(shape, jnp.float32)
    lax.fori_loop(0, levels, forward, (zeros, zeros, (zeros,) * comps), unroll=4)

    def backward(step, following):
        k = levels - 1 - step
        ratio = ratio_ref[k]
        results = []
        for c in range(comps):
            result = outs[c][k] + ratio * following[c]
            outs[c][k] = result
            results.append(result)
        return tuple(results)

    lax.fori_loop(0, levels, backward, (zeros,) * comps, unroll=4)


def solve_columns(provisional, mixing, wet_mask, thickness):
    return pl.pallas_call(
        solve_kernel,
        out_shape=[jax.ShapeDtypeStruct((2,) + provisional.shape[1:], jnp.float32)] * 2,
        in_specs=[pl.BlockSpec(memory_space=pltpu.SMEM)]
        + [pl.BlockSpec(memory_space=pltpu.VMEM)] * 3,
        out_specs=[pl.BlockSpec(memory_space=pltpu.VMEM)] * 2,
        scratch_shapes=[pltpu.VMEM(mixing.shape, jnp.float32)],
    )(thickness, provisional, mixing, wet_mask)


def solution(mesh):
    return jax.shard_map(
        shards,
        mesh=mesh,
        in_specs=(
            P(None, None, ("gy", "ga"), "gx"),
            P(None, None, ("gy", "ga"), "gx"),
            P(None, ("gy", "ga"), "gx"),
            P(),
            P(("gy", "ga")),
            P(("gy", "ga"), "gx"),
            P(("gy", "ga"), "gx"),
            P(("gy", "ga"), "gx"),
            P(None, ("gy", "ga"), "gx"),
        ),
        out_specs=(
            P(None, None, ("gy", "ga"), "gx"),
            P(None, None, ("gy", "ga"), "gx"),
            P(("gy", "ga"), "gx"),
            P(None, ("gy", "ga"), "gx"),
        ),
        check_vma=False,
    )
```

```python
import jax
import jax.numpy as jnp
from jax import lax
from jax.sharding import PartitionSpec as P
from jax.experimental import pallas as pl
from jax.experimental.pallas import tpu as pltpu

NSUB = 30


step_main = 0.1
visc_four = 0.02
diff_four = 0.02
press_scale = 0.02
step_baro = 0.1
grav_baro = 25.0
expand_temp = 0.2
contract_salt = 0.1


def laplace(quantity, wet_mask):
    centre = quantity[..., 1:-1, 1:-1]
    beside_all = (
        quantity[..., 1:-1, 2:]
        + quantity[..., 1:-1, :-2]
        + quantity[..., 2:, 1:-1]
        + quantity[..., :-2, 1:-1]
    )
    return (beside_all - 4.0 * centre) * wet_mask[..., 1:-1, 1:-1]


def diff_x(quantity):
    return 0.5 * (quantity[..., 2:-2, 3:-1] - quantity[..., 2:-2, 1:-3])


def diff_y(quantity):
    return 0.5 * (quantity[..., 3:-1, 2:-2] - quantity[..., 1:-3, 2:-2])


def tendency(padded, pressure, coriolis):
    east_vel = padded[0]
    north_vel = padded[1]
    wet_mask = padded[4]
    inner_wet = wet_mask[..., 2:-2, 2:-2]
    rotate = coriolis[:, None]
    changes = []
    for component in range(4):
        quantity = padded[component]
        advect = diff_x(east_vel * quantity) + diff_y(north_vel * quantity)
        smooth = laplace(laplace(quantity, wet_mask), wet_mask[..., 1:-1, 1:-1])
        if component == 0:
            change = rotate * north_vel[..., 2:-2, 2:-2] - diff_x(pressure) - visc_four * smooth
        elif component == 1:
            change = -rotate * east_vel[..., 2:-2, 2:-2] - diff_y(pressure) - visc_four * smooth
        else:
            change = -diff_four * smooth
        changes.append((change - advect) * inner_wet)
    return jnp.stack(changes)


def vertical_solve(provisional, mixing, wet_mask, thickness):
    levels = thickness.shape[0]
    tail_ones = (1,) * (mixing.ndim - 1)
    depth_col = thickness.reshape((levels,) + tail_ones)
    middle = (0.5 * (thickness[:-1] + thickness[1:])).reshape((levels - 1,) + tail_ones)
    coupling = mixing[:-1] * wet_mask[:-1] * wet_mask[1:] / middle
    zeros_row = jnp.zeros((1,) + mixing.shape[1:], jnp.float32)
    below_link = jnp.concatenate([coupling, zeros_row], axis=0)
    upper_link = jnp.concatenate([zeros_row, coupling], axis=0)
    diagonal = depth_col + upper_link + below_link
    source = depth_col[:, None] * provisional

    def forward(sweep, inputs):
        ratio_prev, value_prev = sweep
        upper_now, diag_now, below_now, source_now = inputs
        divisor = diag_now - upper_now * ratio_prev
        sweep_ratio = below_now / divisor
        sweep_value = (source_now + upper_now[None] * value_prev) / divisor[None]
        return ((sweep_ratio, sweep_value), (sweep_ratio, sweep_value))

    start_sweep = (
        jnp.zeros(mixing.shape[1:], jnp.float32),
        jnp.zeros(provisional.shape[1:], jnp.float32),
    )
    unused, (ratios, values) = lax.scan(
        forward, start_sweep, (upper_link, diagonal, below_link, source)
    )

    def backward(following, inputs):
        sweep_ratio, sweep_value = inputs
        result = sweep_value + sweep_ratio[None] * following
        return (result, result)

    unused_last, solved = lax.scan(
        backward, jnp.zeros(provisional.shape[1:], jnp.float32), (ratios, values), reverse=True
    )
    return solved


def zero_diff(quantity, along):
    extent = quantity.shape[along]
    ahead_part = lax.slice_in_dim(quantity, 1, extent, axis=along)
    behind = lax.slice_in_dim(quantity, 0, extent - 1, axis=along)
    zeros_row = jnp.zeros_like(lax.slice_in_dim(quantity, 0, 1, axis=along))
    return 0.5 * (
        jnp.concatenate([ahead_part, zeros_row], axis=along)
        - jnp.concatenate([zeros_row, behind], axis=along)
    )


def east_zero(quantity):
    return zero_diff(quantity, quantity.ndim - 1)


def north_zero(quantity):
    return zero_diff(quantity, quantity.ndim - 2)


def baro_step(baro_state, statics, east_diff, north_diff):
    height = baro_state[0]
    east_vel = baro_state[1]
    north_vel = baro_state[2]
    depth_ratio = statics[0]
    sea_mask = statics[1]
    rotate = statics[2]
    push_east = statics[3]
    push_north = statics[4]
    new_height = (
        height
        - step_baro * (east_diff(depth_ratio * east_vel) + north_diff(depth_ratio * north_vel))
    ) * sea_mask
    new_east = (
        east_vel + step_baro * (push_east + rotate * north_vel - grav_baro * east_diff(new_height))
    ) * sea_mask
    new_north = (
        north_vel
        + step_baro * (push_north - rotate * east_vel - grav_baro * north_diff(new_height))
    ) * sea_mask
    return jnp.stack([new_height, new_east, new_north])


def halo_3d(block):
    zonal = "gx"
    merid = ("gy", "ga")
    both = ("gx", "gy", "ga")
    zonal_n = lax.axis_size(zonal)
    merid_n = lax.axis_size(merid)

    def send(piece, d_zonal, d_merid):
        if d_merid == 0:
            pairs = [(g, (g + d_zonal) % zonal_n) for g in range(zonal_n)]
            return lax.ppermute(piece, zonal, pairs)
        pairs = []
        for g in range(zonal_n):
            for m in range(merid_n):
                target = m + d_merid
                if 0 <= target < merid_n:
                    pairs.append((g * merid_n + m, ((g + d_zonal) % zonal_n) * merid_n + target))
        if d_zonal == 0:
            return lax.ppermute(piece, merid, [(s % merid_n, t % merid_n) for s, t in pairs[:merid_n - 1]])
        return lax.ppermute(piece, both, pairs)

    w = 2
    last_rows = block[..., -w:, :]
    first_rows = block[..., :w, :]
    west = send(block[..., -w:], 1, 0)
    east = send(block[..., :w], -1, 0)
    low = send(last_rows, 0, 1)
    high = send(first_rows, 0, -1)
    low_west = send(last_rows[..., -w:], 1, 1)
    low_east = send(last_rows[..., :w], -1, 1)
    high_west = send(first_rows[..., -w:], 1, -1)
    high_east = send(first_rows[..., :w], -1, -1)
    low_band = jnp.concatenate([low_west, low, low_east], axis=-1)
    middle = jnp.concatenate([west, block, east], axis=-1)
    high_band = jnp.concatenate([high_west, high, high_east], axis=-1)
    return jnp.concatenate([low_band, middle, high_band], axis=-2)


def shards(velocity, tracers, mixing, thickness, coriolis, land, bottom, surface, barotropic):
    levels = thickness.shape[0]
    land_f = land.astype(jnp.float32)
    level_ids = lax.broadcasted_iota(jnp.int32, (levels,) + land.shape, 0)
    wet_mask = land_f[None] * (level_ids < bottom[None]).astype(jnp.float32)
    stacked = jnp.concatenate(
        [velocity * wet_mask[None], tracers * wet_mask[None], wet_mask[None]], axis=0
    )
    padded = halo_3d(stacked)
    depth_col = thickness.reshape((levels, 1, 1))
    pressure = pressure_run(thickness, padded)
    growth = tendency(padded, pressure, coriolis)
    provisional = stacked[:4] + step_main * growth
    forcing = jnp.sum(depth_col * growth[:2], axis=1)
    depth_sum = jnp.sum(depth_col * wet_mask, axis=0)
    safe_depth = jnp.maximum(depth_sum, 1.0)
    dr = depth_sum / jnp.sum(thickness)
    push_u = forcing[0] / safe_depth * land_f
    push_v = forcing[1] / safe_depth * land_f
    rotate = coriolis[:, None] * jnp.ones_like(land_f)
    fields = jnp.stack([dr, land_f, rotate, push_u, push_v, surface, barotropic[0], barotropic[1]])
    whole = gather_baro(fields)
    rows = land.shape[0]
    row_offset = jnp.full((1,), lax.axis_index(("gy", "ga")) * rows, jnp.int32)
    new_surface, new_barotropic, average = baro_run(whole, row_offset, land.shape[1])
    solved = solve_columns(provisional, mixing, wet_mask, thickness)
    thick_col = thickness.reshape((levels, 1, 1))
    depth_mean = jnp.sum(thick_col[None] * wet_mask[None] * solved[:2], axis=1) / safe_depth
    new_velocity = (solved[:2] - depth_mean[:, None] + average[:, None]) * wet_mask[None]
    new_tracers = solved[2:]
    return (new_velocity, new_tracers, new_surface, new_barotropic)


BARO_HALO = 64


def gather_baro(fields):
    count = lax.axis_size("gx")
    forward = [(i, (i + 1) % count) for i in range(count)]
    backward = [(target, source) for source, target in forward]
    low = lax.ppermute(fields[..., -BARO_HALO:], "gx", forward)
    high = lax.ppermute(fields[..., :BARO_HALO], "gx", backward)
    wide = jnp.concatenate([low, fields, high], axis=-1)
    merid = ("gy", "ga")
    parts = lax.axis_size(merid)
    blocks = [wide]
    for shift in range(1, parts):
        pairs = [(d, (d - shift) % parts) for d in range(parts)]
        blocks.append(lax.ppermute(wide, merid, pairs))
    return jnp.stack(blocks)


def baro_kernel(off_ref, f_ref, eta_ref, vel_ref, avg_ref):
    parts = f_ref.shape[0]
    block_rows = f_ref.shape[2]
    rows = parts * block_rows
    cols = f_ref.shape[3]

    def field(index):
        return jnp.concatenate([f_ref[part, index] for part in range(parts)], axis=0)

    depth_ratio = field(0)
    sea_mask = field(1)
    rotate = field(2)
    push_east = field(3)
    push_north = field(4)
    offset = off_ref[0]
    last_local = rows - 1 - offset
    first_local = jnp.where(offset == 0, 0, rows - offset)
    row = lax.broadcasted_iota(jnp.int32, (rows, cols), 0)
    not_last = row != last_local
    not_first = row != first_local

    def east_diff(q):
        return 0.5 * (pltpu.roll(q, cols - 1, 1) - pltpu.roll(q, 1, 1))

    def north_diff(q):
        ahead = jnp.where(not_last, pltpu.roll(q, rows - 1, 0), 0.0)
        behind = jnp.where(not_first, pltpu.roll(q, 1, 0), 0.0)
        return 0.5 * (ahead - behind)

    def body(turn, carry):
        height, east_vel, north_vel, sum_east, sum_north = carry
        height = (
            height
            - step_baro * (east_diff(depth_ratio * east_vel) + north_diff(depth_ratio * north_vel))
        ) * sea_mask
        new_east = (
            east_vel + step_baro * (push_east + rotate * north_vel - grav_baro * east_diff(height))
        ) * sea_mask
        new_north = (
            north_vel
            + step_baro * (push_north - rotate * east_vel - grav_baro * north_diff(height))
        ) * sea_mask
        return (height, new_east, new_north, sum_east + new_east, sum_north + new_north)

    zeros = jnp.zeros((rows, cols), jnp.float32)
    carry = (field(5), field(6), field(7), zeros, zeros)
    height, east_vel, north_vel, sum_east, sum_north = lax.fori_loop(0, NSUB, body, carry)
    finals = (height, east_vel, north_vel, sum_east / NSUB, sum_north / NSUB)
    out_cols = eta_ref.shape[1]
    targets = [eta_ref, vel_ref.at[0], vel_ref.at[1], avg_ref.at[0], avg_ref.at[1]]
    for index in range(5):
        targets[index][...] = pltpu.roll(finals[index][:block_rows], cols - BARO_HALO, 1)[:, :out_cols]


def baro_run(whole, row_offset, out_cols):
    return pl.pallas_call(
        baro_kernel,
        out_shape=[
            jax.ShapeDtypeStruct((whole.shape[2], out_cols), jnp.float32),
            jax.ShapeDtypeStruct((2, whole.shape[2], out_cols), jnp.float32),
            jax.ShapeDtypeStruct((2, whole.shape[2], out_cols), jnp.float32),
        ],
        in_specs=[pl.BlockSpec(memory_space=pltpu.SMEM), pl.BlockSpec(memory_space=pltpu.VMEM)],
        out_specs=[pl.BlockSpec(memory_space=pltpu.VMEM)] * 3,
    )(row_offset, whole)


def pressure_kernel(th_ref, pad_ref, o_ref):
    levels = pad_ref.shape[1]

    def body(k, overlying):
        weight = (contract_salt * pad_ref[3, k] - expand_temp * pad_ref[2, k]) * pad_ref[4, k] * th_ref[k]
        o_ref[k] = press_scale * (overlying + 0.5 * weight)
        return overlying + weight

    lax.fori_loop(0, levels, body, jnp.zeros(pad_ref.shape[2:], jnp.float32), unroll=8)


def pressure_run(thickness, padded):
    return pl.pallas_call(
        pressure_kernel,
        out_shape=jax.ShapeDtypeStruct(padded.shape[1:], jnp.float32),
        in_specs=[pl.BlockSpec(memory_space=pltpu.SMEM), pl.BlockSpec(memory_space=pltpu.VMEM)],
        out_specs=pl.BlockSpec(memory_space=pltpu.VMEM),
    )(thickness, padded)


def solve_kernel(th_ref, prov_ref, mix_ref, wet_ref, o_ref, ratio_ref):
    levels = mix_ref.shape[0]
    shape = mix_ref.shape[1:]
    comps = prov_ref.shape[0]

    def below_of(k):
        nxt = jnp.minimum(k + 1, levels - 1)
        middle = 0.5 * (th_ref[k] + th_ref[nxt])
        coupling = mix_ref[k] * wet_ref[k] * wet_ref[nxt] / middle
        return jnp.where(k < levels - 1, coupling, 0.0)

    def forward(k, carry):
        upper, ratio_prev, value_prev = carry
        below = below_of(k)
        depth = th_ref[k]
        diagonal = depth + upper + below
        divisor = diagonal - upper * ratio_prev
        inverse = 1.0 / divisor
        ratio = below * inverse
        ratio_ref[k] = ratio
        values = []
        for c in range(comps):
            value = (depth * prov_ref[c, k] + upper * value_prev[c]) * inverse
            o_ref[c, k] = value
            values.append(value)
        return (below, ratio, tuple(values))

    zeros = jnp.zeros(shape, jnp.float32)
    lax.fori_loop(0, levels, forward, (zeros, zeros, (zeros,) * comps), unroll=4)

    def backward(step, following):
        k = levels - 1 - step
        ratio = ratio_ref[k]
        results = []
        for c in range(comps):
            result = o_ref[c, k] + ratio * following[c]
            o_ref[c, k] = result
            results.append(result)
        return tuple(results)

    lax.fori_loop(0, levels, backward, (zeros,) * comps, unroll=4)


def solve_columns(provisional, mixing, wet_mask, thickness):
    return pl.pallas_call(
        solve_kernel,
        out_shape=jax.ShapeDtypeStruct(provisional.shape, jnp.float32),
        in_specs=[pl.BlockSpec(memory_space=pltpu.SMEM)]
        + [pl.BlockSpec(memory_space=pltpu.VMEM)] * 3,
        out_specs=pl.BlockSpec(memory_space=pltpu.VMEM),
        scratch_shapes=[pltpu.VMEM(mixing.shape, jnp.float32)],
    )(thickness, provisional, mixing, wet_mask)


def solution(mesh):
    return jax.shard_map(
        shards,
        mesh=mesh,
        in_specs=(
            P(None, None, ("gy", "ga"), "gx"),
            P(None, None, ("gy", "ga"), "gx"),
            P(None, ("gy", "ga"), "gx"),
            P(),
            P(("gy", "ga")),
            P(("gy", "ga"), "gx"),
            P(("gy", "ga"), "gx"),
            P(("gy", "ga"), "gx"),
            P(None, ("gy", "ga"), "gx"),
        ),
        out_specs=(
            P(None, None, ("gy", "ga"), "gx"),
            P(None, None, ("gy", "ga"), "gx"),
            P(("gy", "ga"), "gx"),
            P(None, ("gy", "ga"), "gx"),
        ),
        check_vma=False,
    )
```

```python
import jax
import jax.numpy as jnp
from jax import lax
from jax.sharding import PartitionSpec as P
from jax.experimental import pallas as pl
from jax.experimental.pallas import tpu as pltpu

NSUB = 30


step_main = 0.1
visc_four = 0.02
diff_four = 0.02
press_scale = 0.02
step_baro = 0.1
grav_baro = 25.0
expand_temp = 0.2
contract_salt = 0.1


def laplace(quantity, wet_mask):
    centre = quantity[..., 1:-1, 1:-1]
    beside_all = (
        quantity[..., 1:-1, 2:]
        + quantity[..., 1:-1, :-2]
        + quantity[..., 2:, 1:-1]
        + quantity[..., :-2, 1:-1]
    )
    return (beside_all - 4.0 * centre) * wet_mask[..., 1:-1, 1:-1]


def diff_x(quantity):
    return 0.5 * (quantity[..., 2:-2, 3:-1] - quantity[..., 2:-2, 1:-3])


def diff_y(quantity):
    return 0.5 * (quantity[..., 3:-1, 2:-2] - quantity[..., 1:-3, 2:-2])


def tendency(padded, pressure, coriolis):
    east_vel = padded[0]
    north_vel = padded[1]
    wet_mask = padded[4]
    inner_wet = wet_mask[..., 2:-2, 2:-2]
    rotate = coriolis[:, None]
    changes = []
    for component in range(4):
        quantity = padded[component]
        advect = diff_x(east_vel * quantity) + diff_y(north_vel * quantity)
        smooth = laplace(laplace(quantity, wet_mask), wet_mask[..., 1:-1, 1:-1])
        if component == 0:
            change = rotate * north_vel[..., 2:-2, 2:-2] - diff_x(pressure) - visc_four * smooth
        elif component == 1:
            change = -rotate * east_vel[..., 2:-2, 2:-2] - diff_y(pressure) - visc_four * smooth
        else:
            change = -diff_four * smooth
        changes.append((change - advect) * inner_wet)
    return jnp.stack(changes)


def vertical_solve(provisional, mixing, wet_mask, thickness):
    levels = thickness.shape[0]
    tail_ones = (1,) * (mixing.ndim - 1)
    depth_col = thickness.reshape((levels,) + tail_ones)
    middle = (0.5 * (thickness[:-1] + thickness[1:])).reshape((levels - 1,) + tail_ones)
    coupling = mixing[:-1] * wet_mask[:-1] * wet_mask[1:] / middle
    zeros_row = jnp.zeros((1,) + mixing.shape[1:], jnp.float32)
    below_link = jnp.concatenate([coupling, zeros_row], axis=0)
    upper_link = jnp.concatenate([zeros_row, coupling], axis=0)
    diagonal = depth_col + upper_link + below_link
    source = depth_col[:, None] * provisional

    def forward(sweep, inputs):
        ratio_prev, value_prev = sweep
        upper_now, diag_now, below_now, source_now = inputs
        divisor = diag_now - upper_now * ratio_prev
        sweep_ratio = below_now / divisor
        sweep_value = (source_now + upper_now[None] * value_prev) / divisor[None]
        return ((sweep_ratio, sweep_value), (sweep_ratio, sweep_value))

    start_sweep = (
        jnp.zeros(mixing.shape[1:], jnp.float32),
        jnp.zeros(provisional.shape[1:], jnp.float32),
    )
    unused, (ratios, values) = lax.scan(
        forward, start_sweep, (upper_link, diagonal, below_link, source)
    )

    def backward(following, inputs):
        sweep_ratio, sweep_value = inputs
        result = sweep_value + sweep_ratio[None] * following
        return (result, result)

    unused_last, solved = lax.scan(
        backward, jnp.zeros(provisional.shape[1:], jnp.float32), (ratios, values), reverse=True
    )
    return solved


def zero_diff(quantity, along):
    extent = quantity.shape[along]
    ahead_part = lax.slice_in_dim(quantity, 1, extent, axis=along)
    behind = lax.slice_in_dim(quantity, 0, extent - 1, axis=along)
    zeros_row = jnp.zeros_like(lax.slice_in_dim(quantity, 0, 1, axis=along))
    return 0.5 * (
        jnp.concatenate([ahead_part, zeros_row], axis=along)
        - jnp.concatenate([zeros_row, behind], axis=along)
    )


def east_zero(quantity):
    return zero_diff(quantity, quantity.ndim - 1)


def north_zero(quantity):
    return zero_diff(quantity, quantity.ndim - 2)


def baro_step(baro_state, statics, east_diff, north_diff):
    height = baro_state[0]
    east_vel = baro_state[1]
    north_vel = baro_state[2]
    depth_ratio = statics[0]
    sea_mask = statics[1]
    rotate = statics[2]
    push_east = statics[3]
    push_north = statics[4]
    new_height = (
        height
        - step_baro * (east_diff(depth_ratio * east_vel) + north_diff(depth_ratio * north_vel))
    ) * sea_mask
    new_east = (
        east_vel + step_baro * (push_east + rotate * north_vel - grav_baro * east_diff(new_height))
    ) * sea_mask
    new_north = (
        north_vel
        + step_baro * (push_north - rotate * east_vel - grav_baro * north_diff(new_height))
    ) * sea_mask
    return jnp.stack([new_height, new_east, new_north])


def halo_3d(block):
    zonal = "gx"
    merid = ("gy", "ga")
    both = ("gx", "gy", "ga")
    zonal_n = lax.axis_size(zonal)
    merid_n = lax.axis_size(merid)

    def send(piece, d_zonal, d_merid):
        if d_merid == 0:
            pairs = [(g, (g + d_zonal) % zonal_n) for g in range(zonal_n)]
            return lax.ppermute(piece, zonal, pairs)
        pairs = []
        for g in range(zonal_n):
            for m in range(merid_n):
                target = m + d_merid
                if 0 <= target < merid_n:
                    pairs.append((g * merid_n + m, ((g + d_zonal) % zonal_n) * merid_n + target))
        if d_zonal == 0:
            return lax.ppermute(piece, merid, [(s % merid_n, t % merid_n) for s, t in pairs[:merid_n - 1]])
        return lax.ppermute(piece, both, pairs)

    w = 2
    last_rows = block[..., -w:, :]
    first_rows = block[..., :w, :]
    west = send(block[..., -w:], 1, 0)
    east = send(block[..., :w], -1, 0)
    low = send(last_rows, 0, 1)
    high = send(first_rows, 0, -1)
    low_west = send(last_rows[..., -w:], 1, 1)
    low_east = send(last_rows[..., :w], -1, 1)
    high_west = send(first_rows[..., -w:], 1, -1)
    high_east = send(first_rows[..., :w], -1, -1)
    low_band = jnp.concatenate([low_west, low, low_east], axis=-1)
    middle = jnp.concatenate([west, block, east], axis=-1)
    high_band = jnp.concatenate([high_west, high, high_east], axis=-1)
    return jnp.concatenate([low_band, middle, high_band], axis=-2)


def shards(velocity, tracers, mixing, thickness, coriolis, land, bottom, surface, barotropic):
    levels = thickness.shape[0]
    land_f = land.astype(jnp.float32)
    level_ids = lax.broadcasted_iota(jnp.int32, (levels,) + land.shape, 0)
    wet_mask = land_f[None] * (level_ids < bottom[None]).astype(jnp.float32)
    stacked = jnp.concatenate(
        [velocity * wet_mask[None], tracers * wet_mask[None], wet_mask[None]], axis=0
    )
    padded = halo_3d(stacked)
    depth_col = thickness.reshape((levels, 1, 1))
    pressure = pressure_run(thickness, padded)
    growth = tendency(padded, pressure, coriolis)
    provisional = stacked[:4] + step_main * growth
    forcing = jnp.sum(depth_col * growth[:2], axis=1)
    depth_sum = jnp.sum(depth_col * wet_mask, axis=0)
    safe_depth = jnp.maximum(depth_sum, 1.0)
    dr = depth_sum / jnp.sum(thickness)
    push_u = forcing[0] / safe_depth * land_f
    push_v = forcing[1] / safe_depth * land_f
    rotate = coriolis[:, None] * jnp.ones_like(land_f)
    fields = jnp.stack([dr, land_f, rotate, push_u, push_v, surface, barotropic[0], barotropic[1]])
    whole = gather_baro(fields)
    rows = land.shape[0]
    row_offset = jnp.full((1,), lax.axis_index(("gy", "ga")) * rows, jnp.int32)
    new_surface, new_barotropic, average = baro_run(whole, row_offset, land.shape[1])
    solved = solve_columns(provisional, mixing, wet_mask, thickness)
    thick_col = thickness.reshape((levels, 1, 1))
    depth_mean = jnp.sum(thick_col[None] * wet_mask[None] * solved[:2], axis=1) / safe_depth
    new_velocity = (solved[:2] - depth_mean[:, None] + average[:, None]) * wet_mask[None]
    new_tracers = solved[2:]
    return (new_velocity, new_tracers, new_surface, new_barotropic)


BARO_HALO = 64


def gather_baro(fields):
    count = lax.axis_size("gx")
    forward = [(i, (i + 1) % count) for i in range(count)]
    backward = [(target, source) for source, target in forward]
    low = lax.ppermute(fields[..., -BARO_HALO:], "gx", forward)
    high = lax.ppermute(fields[..., :BARO_HALO], "gx", backward)
    wide = jnp.concatenate([low, fields, high], axis=-1)
    merid = ("gy", "ga")
    parts = lax.axis_size(merid)
    blocks = [wide]
    for shift in range(1, parts):
        pairs = [(d, (d - shift) % parts) for d in range(parts)]
        blocks.append(lax.ppermute(wide, merid, pairs))
    return jnp.stack(blocks)


def baro_kernel(off_ref, f_ref, eta_ref, vel_ref, avg_ref):
    parts = f_ref.shape[0]
    block_rows = f_ref.shape[2]
    rows = parts * block_rows
    cols = f_ref.shape[3]

    def field(index):
        return jnp.concatenate([f_ref[part, index] for part in range(parts)], axis=0)

    depth_ratio = field(0)
    sea_mask = field(1)
    rotate = field(2)
    push_east = field(3)
    push_north = field(4)
    offset = off_ref[0]
    last_local = rows - 1 - offset
    first_local = jnp.where(offset == 0, 0, rows - offset)
    row = lax.broadcasted_iota(jnp.int32, (rows, cols), 0)
    not_last = row != last_local
    not_first = row != first_local

    def east_diff(q):
        return 0.5 * (pltpu.roll(q, cols - 1, 1) - pltpu.roll(q, 1, 1))

    def north_diff(q):
        ahead = jnp.where(not_last, pltpu.roll(q, rows - 1, 0), 0.0)
        behind = jnp.where(not_first, pltpu.roll(q, 1, 0), 0.0)
        return 0.5 * (ahead - behind)

    def body(turn, carry):
        height, east_vel, north_vel, sum_east, sum_north = carry
        height = (
            height
            - step_baro * (east_diff(depth_ratio * east_vel) + north_diff(depth_ratio * north_vel))
        ) * sea_mask
        new_east = (
            east_vel + step_baro * (push_east + rotate * north_vel - grav_baro * east_diff(height))
        ) * sea_mask
        new_north = (
            north_vel
            + step_baro * (push_north - rotate * east_vel - grav_baro * north_diff(height))
        ) * sea_mask
        return (height, new_east, new_north, sum_east + new_east, sum_north + new_north)

    zeros = jnp.zeros((rows, cols), jnp.float32)
    carry = (field(5), field(6), field(7), zeros, zeros)
    height, east_vel, north_vel, sum_east, sum_north = lax.fori_loop(0, NSUB, body, carry, unroll=2)
    finals = (height, east_vel, north_vel, sum_east / NSUB, sum_north / NSUB)
    out_cols = eta_ref.shape[1]
    targets = [eta_ref, vel_ref.at[0], vel_ref.at[1], avg_ref.at[0], avg_ref.at[1]]
    for index in range(5):
        targets[index][...] = pltpu.roll(finals[index][:block_rows], cols - BARO_HALO, 1)[:, :out_cols]


def baro_run(whole, row_offset, out_cols):
    return pl.pallas_call(
        baro_kernel,
        out_shape=[
            jax.ShapeDtypeStruct((whole.shape[2], out_cols), jnp.float32),
            jax.ShapeDtypeStruct((2, whole.shape[2], out_cols), jnp.float32),
            jax.ShapeDtypeStruct((2, whole.shape[2], out_cols), jnp.float32),
        ],
        in_specs=[pl.BlockSpec(memory_space=pltpu.SMEM), pl.BlockSpec(memory_space=pltpu.VMEM)],
        out_specs=[pl.BlockSpec(memory_space=pltpu.VMEM)] * 3,
    )(row_offset, whole)


def pressure_kernel(th_ref, pad_ref, o_ref):
    levels = pad_ref.shape[1]

    def body(k, overlying):
        weight = (contract_salt * pad_ref[3, k] - expand_temp * pad_ref[2, k]) * pad_ref[4, k] * th_ref[k]
        o_ref[k] = press_scale * (overlying + 0.5 * weight)
        return overlying + weight

    lax.fori_loop(0, levels, body, jnp.zeros(pad_ref.shape[2:], jnp.float32), unroll=8)


def pressure_run(thickness, padded):
    return pl.pallas_call(
        pressure_kernel,
        out_shape=jax.ShapeDtypeStruct(padded.shape[1:], jnp.float32),
        in_specs=[pl.BlockSpec(memory_space=pltpu.SMEM), pl.BlockSpec(memory_space=pltpu.VMEM)],
        out_specs=pl.BlockSpec(memory_space=pltpu.VMEM),
    )(thickness, padded)


def solve_kernel(th_ref, prov_ref, mix_ref, wet_ref, o_ref, ratio_ref):
    levels = mix_ref.shape[0]
    shape = mix_ref.shape[1:]
    comps = prov_ref.shape[0]

    def below_of(k):
        nxt = jnp.minimum(k + 1, levels - 1)
        middle = 0.5 * (th_ref[k] + th_ref[nxt])
        coupling = mix_ref[k] * wet_ref[k] * wet_ref[nxt] / middle
        return jnp.where(k < levels - 1, coupling, 0.0)

    def forward(k, carry):
        upper, ratio_prev, value_prev = carry
        below = below_of(k)
        depth = th_ref[k]
        diagonal = depth + upper + below
        divisor = diagonal - upper * ratio_prev
        inverse = 1.0 / divisor
        ratio = below * inverse
        ratio_ref[k] = ratio
        values = []
        for c in range(comps):
            value = (depth * prov_ref[c, k] + upper * value_prev[c]) * inverse
            o_ref[c, k] = value
            values.append(value)
        return (below, ratio, tuple(values))

    zeros = jnp.zeros(shape, jnp.float32)
    lax.fori_loop(0, levels, forward, (zeros, zeros, (zeros,) * comps), unroll=4)

    def backward(step, following):
        k = levels - 1 - step
        ratio = ratio_ref[k]
        results = []
        for c in range(comps):
            result = o_ref[c, k] + ratio * following[c]
            o_ref[c, k] = result
            results.append(result)
        return tuple(results)

    lax.fori_loop(0, levels, backward, (zeros,) * comps, unroll=4)


def solve_columns(provisional, mixing, wet_mask, thickness):
    return pl.pallas_call(
        solve_kernel,
        out_shape=jax.ShapeDtypeStruct(provisional.shape, jnp.float32),
        in_specs=[pl.BlockSpec(memory_space=pltpu.SMEM)]
        + [pl.BlockSpec(memory_space=pltpu.VMEM)] * 3,
        out_specs=pl.BlockSpec(memory_space=pltpu.VMEM),
        scratch_shapes=[pltpu.VMEM(mixing.shape, jnp.float32)],
    )(thickness, provisional, mixing, wet_mask)


def solution(mesh):
    return jax.shard_map(
        shards,
        mesh=mesh,
        in_specs=(
            P(None, None, ("gy", "ga"), "gx"),
            P(None, None, ("gy", "ga"), "gx"),
            P(None, ("gy", "ga"), "gx"),
            P(),
            P(("gy", "ga")),
            P(("gy", "ga"), "gx"),
            P(("gy", "ga"), "gx"),
            P(("gy", "ga"), "gx"),
            P(None, ("gy", "ga"), "gx"),
        ),
        out_specs=(
            P(None, None, ("gy", "ga"), "gx"),
            P(None, None, ("gy", "ga"), "gx"),
            P(("gy", "ga"), "gx"),
            P(None, ("gy", "ga"), "gx"),
        ),
        check_vma=False,
    )
```

```python
import jax
import jax.numpy as jnp
from jax import lax
from jax.sharding import PartitionSpec as P
from jax.experimental import pallas as pl
from jax.experimental.pallas import tpu as pltpu

NSUB = 30


step_main = 0.1
visc_four = 0.02
diff_four = 0.02
press_scale = 0.02
step_baro = 0.1
grav_baro = 25.0
expand_temp = 0.2
contract_salt = 0.1


def laplace(quantity, wet_mask):
    centre = quantity[..., 1:-1, 1:-1]
    beside_all = (
        quantity[..., 1:-1, 2:]
        + quantity[..., 1:-1, :-2]
        + quantity[..., 2:, 1:-1]
        + quantity[..., :-2, 1:-1]
    )
    return (beside_all - 4.0 * centre) * wet_mask[..., 1:-1, 1:-1]


def diff_x(quantity):
    return 0.5 * (quantity[..., 2:-2, 3:-1] - quantity[..., 2:-2, 1:-3])


def diff_y(quantity):
    return 0.5 * (quantity[..., 3:-1, 2:-2] - quantity[..., 1:-3, 2:-2])


def tendency(padded, pressure, coriolis):
    east_vel = padded[0]
    north_vel = padded[1]
    wet_mask = padded[4]
    inner_wet = wet_mask[..., 2:-2, 2:-2]
    rotate = coriolis[:, None]
    changes = []
    for component in range(4):
        quantity = padded[component]
        advect = diff_x(east_vel * quantity) + diff_y(north_vel * quantity)
        smooth = laplace(laplace(quantity, wet_mask), wet_mask[..., 1:-1, 1:-1])
        if component == 0:
            change = rotate * north_vel[..., 2:-2, 2:-2] - diff_x(pressure) - visc_four * smooth
        elif component == 1:
            change = -rotate * east_vel[..., 2:-2, 2:-2] - diff_y(pressure) - visc_four * smooth
        else:
            change = -diff_four * smooth
        changes.append((change - advect) * inner_wet)
    return changes


def vertical_solve(provisional, mixing, wet_mask, thickness):
    levels = thickness.shape[0]
    tail_ones = (1,) * (mixing.ndim - 1)
    depth_col = thickness.reshape((levels,) + tail_ones)
    middle = (0.5 * (thickness[:-1] + thickness[1:])).reshape((levels - 1,) + tail_ones)
    coupling = mixing[:-1] * wet_mask[:-1] * wet_mask[1:] / middle
    zeros_row = jnp.zeros((1,) + mixing.shape[1:], jnp.float32)
    below_link = jnp.concatenate([coupling, zeros_row], axis=0)
    upper_link = jnp.concatenate([zeros_row, coupling], axis=0)
    diagonal = depth_col + upper_link + below_link
    source = depth_col[:, None] * provisional

    def forward(sweep, inputs):
        ratio_prev, value_prev = sweep
        upper_now, diag_now, below_now, source_now = inputs
        divisor = diag_now - upper_now * ratio_prev
        sweep_ratio = below_now / divisor
        sweep_value = (source_now + upper_now[None] * value_prev) / divisor[None]
        return ((sweep_ratio, sweep_value), (sweep_ratio, sweep_value))

    start_sweep = (
        jnp.zeros(mixing.shape[1:], jnp.float32),
        jnp.zeros(provisional.shape[1:], jnp.float32),
    )
    unused, (ratios, values) = lax.scan(
        forward, start_sweep, (upper_link, diagonal, below_link, source)
    )

    def backward(following, inputs):
        sweep_ratio, sweep_value = inputs
        result = sweep_value + sweep_ratio[None] * following
        return (result, result)

    unused_last, solved = lax.scan(
        backward, jnp.zeros(provisional.shape[1:], jnp.float32), (ratios, values), reverse=True
    )
    return solved


def zero_diff(quantity, along):
    extent = quantity.shape[along]
    ahead_part = lax.slice_in_dim(quantity, 1, extent, axis=along)
    behind = lax.slice_in_dim(quantity, 0, extent - 1, axis=along)
    zeros_row = jnp.zeros_like(lax.slice_in_dim(quantity, 0, 1, axis=along))
    return 0.5 * (
        jnp.concatenate([ahead_part, zeros_row], axis=along)
        - jnp.concatenate([zeros_row, behind], axis=along)
    )


def east_zero(quantity):
    return zero_diff(quantity, quantity.ndim - 1)


def north_zero(quantity):
    return zero_diff(quantity, quantity.ndim - 2)


def baro_step(baro_state, statics, east_diff, north_diff):
    height = baro_state[0]
    east_vel = baro_state[1]
    north_vel = baro_state[2]
    depth_ratio = statics[0]
    sea_mask = statics[1]
    rotate = statics[2]
    push_east = statics[3]
    push_north = statics[4]
    new_height = (
        height
        - step_baro * (east_diff(depth_ratio * east_vel) + north_diff(depth_ratio * north_vel))
    ) * sea_mask
    new_east = (
        east_vel + step_baro * (push_east + rotate * north_vel - grav_baro * east_diff(new_height))
    ) * sea_mask
    new_north = (
        north_vel
        + step_baro * (push_north - rotate * east_vel - grav_baro * north_diff(new_height))
    ) * sea_mask
    return jnp.stack([new_height, new_east, new_north])


def halo_3d(block):
    zonal = "gx"
    merid = ("gy", "ga")
    both = ("gx", "gy", "ga")
    zonal_n = lax.axis_size(zonal)
    merid_n = lax.axis_size(merid)

    def send(piece, d_zonal, d_merid):
        if d_merid == 0:
            pairs = [(g, (g + d_zonal) % zonal_n) for g in range(zonal_n)]
            return lax.ppermute(piece, zonal, pairs)
        pairs = []
        for g in range(zonal_n):
            for m in range(merid_n):
                target = m + d_merid
                if 0 <= target < merid_n:
                    pairs.append((g * merid_n + m, ((g + d_zonal) % zonal_n) * merid_n + target))
        if d_zonal == 0:
            return lax.ppermute(piece, merid, [(s % merid_n, t % merid_n) for s, t in pairs[:merid_n - 1]])
        return lax.ppermute(piece, both, pairs)

    w = 2
    last_rows = block[..., -w:, :]
    first_rows = block[..., :w, :]
    west = send(block[..., -w:], 1, 0)
    east = send(block[..., :w], -1, 0)
    low = send(last_rows, 0, 1)
    high = send(first_rows, 0, -1)
    low_west = send(last_rows[..., -w:], 1, 1)
    low_east = send(last_rows[..., :w], -1, 1)
    high_west = send(first_rows[..., -w:], 1, -1)
    high_east = send(first_rows[..., :w], -1, -1)
    low_band = jnp.concatenate([low_west, low, low_east], axis=-1)
    middle = jnp.concatenate([west, block, east], axis=-1)
    high_band = jnp.concatenate([high_west, high, high_east], axis=-1)
    return jnp.concatenate([low_band, middle, high_band], axis=-2)


def shards(velocity, tracers, mixing, thickness, coriolis, land, bottom, surface, barotropic):
    levels = thickness.shape[0]
    land_f = land.astype(jnp.float32)
    level_ids = lax.broadcasted_iota(jnp.int32, (levels,) + land.shape, 0)
    wet_mask = land_f[None] * (level_ids < bottom[None]).astype(jnp.float32)
    stacked = jnp.concatenate(
        [velocity * wet_mask[None], tracers * wet_mask[None], wet_mask[None]], axis=0
    )
    padded = halo_3d(stacked)
    depth_col = thickness.reshape((levels, 1, 1))
    pressure = pressure_run(thickness, padded)
    growth = tendency(padded, pressure, coriolis)
    forcing = jnp.sum(depth_col * jnp.stack(growth[:2]), axis=1)
    depth_sum = jnp.sum(depth_col * wet_mask, axis=0)
    safe_depth = jnp.maximum(depth_sum, 1.0)
    dr = depth_sum / jnp.sum(thickness)
    push_u = forcing[0] / safe_depth * land_f
    push_v = forcing[1] / safe_depth * land_f
    rotate = coriolis[:, None] * jnp.ones_like(land_f)
    fields = jnp.stack([dr, land_f, rotate, push_u, push_v, surface, barotropic[0], barotropic[1]])
    whole = gather_baro(fields)
    rows = land.shape[0]
    row_offset = jnp.full((1,), lax.axis_index(("gy", "ga")) * rows, jnp.int32)
    new_surface, new_barotropic, average = baro_run(whole, row_offset, land.shape[1])
    solved = solve_columns(velocity, tracers, growth, mixing, wet_mask, thickness)
    thick_col = thickness.reshape((levels, 1, 1))
    depth_mean = jnp.sum(thick_col[None] * wet_mask[None] * solved[:2], axis=1) / safe_depth
    new_velocity = (solved[:2] - depth_mean[:, None] + average[:, None]) * wet_mask[None]
    new_tracers = solved[2:]
    return (new_velocity, new_tracers, new_surface, new_barotropic)


BARO_HALO = 64


def gather_baro(fields):
    count = lax.axis_size("gx")
    forward = [(i, (i + 1) % count) for i in range(count)]
    backward = [(target, source) for source, target in forward]
    low = lax.ppermute(fields[..., -BARO_HALO:], "gx", forward)
    high = lax.ppermute(fields[..., :BARO_HALO], "gx", backward)
    wide = jnp.concatenate([low, fields, high], axis=-1)
    merid = ("gy", "ga")
    parts = lax.axis_size(merid)
    blocks = [wide]
    for shift in range(1, parts):
        pairs = [(d, (d - shift) % parts) for d in range(parts)]
        blocks.append(lax.ppermute(wide, merid, pairs))
    return jnp.stack(blocks)


def baro_kernel(off_ref, f_ref, eta_ref, vel_ref, avg_ref):
    parts = f_ref.shape[0]
    block_rows = f_ref.shape[2]
    rows = parts * block_rows
    cols = f_ref.shape[3]

    def field(index):
        return jnp.concatenate([f_ref[part, index] for part in range(parts)], axis=0)

    depth_ratio = field(0)
    sea_mask = field(1)
    rotate = field(2)
    push_east = field(3)
    push_north = field(4)
    offset = off_ref[0]
    last_local = rows - 1 - offset
    first_local = jnp.where(offset == 0, 0, rows - offset)
    row = lax.broadcasted_iota(jnp.int32, (rows, cols), 0)
    not_last = row != last_local
    not_first = row != first_local

    def east_diff(q):
        return 0.5 * (pltpu.roll(q, cols - 1, 1) - pltpu.roll(q, 1, 1))

    def north_diff(q):
        ahead = jnp.where(not_last, pltpu.roll(q, rows - 1, 0), 0.0)
        behind = jnp.where(not_first, pltpu.roll(q, 1, 0), 0.0)
        return 0.5 * (ahead - behind)

    def body(turn, carry):
        height, east_vel, north_vel, sum_east, sum_north = carry
        height = (
            height
            - step_baro * (east_diff(depth_ratio * east_vel) + north_diff(depth_ratio * north_vel))
        ) * sea_mask
        new_east = (
            east_vel + step_baro * (push_east + rotate * north_vel - grav_baro * east_diff(height))
        ) * sea_mask
        new_north = (
            north_vel
            + step_baro * (push_north - rotate * east_vel - grav_baro * north_diff(height))
        ) * sea_mask
        return (height, new_east, new_north, sum_east + new_east, sum_north + new_north)

    zeros = jnp.zeros((rows, cols), jnp.float32)
    carry = (field(5), field(6), field(7), zeros, zeros)
    height, east_vel, north_vel, sum_east, sum_north = lax.fori_loop(0, NSUB, body, carry, unroll=2)
    finals = (height, east_vel, north_vel, sum_east / NSUB, sum_north / NSUB)
    out_cols = eta_ref.shape[1]
    targets = [eta_ref, vel_ref.at[0], vel_ref.at[1], avg_ref.at[0], avg_ref.at[1]]
    for index in range(5):
        targets[index][...] = pltpu.roll(finals[index][:block_rows], cols - BARO_HALO, 1)[:, :out_cols]


def baro_run(whole, row_offset, out_cols):
    return pl.pallas_call(
        baro_kernel,
        out_shape=[
            jax.ShapeDtypeStruct((whole.shape[2], out_cols), jnp.float32),
            jax.ShapeDtypeStruct((2, whole.shape[2], out_cols), jnp.float32),
            jax.ShapeDtypeStruct((2, whole.shape[2], out_cols), jnp.float32),
        ],
        in_specs=[pl.BlockSpec(memory_space=pltpu.SMEM), pl.BlockSpec(memory_space=pltpu.VMEM)],
        out_specs=[pl.BlockSpec(memory_space=pltpu.VMEM)] * 3,
    )(row_offset, whole)


def pressure_kernel(th_ref, pad_ref, o_ref):
    levels = pad_ref.shape[1]

    def body(k, overlying):
        weight = (contract_salt * pad_ref[3, k] - expand_temp * pad_ref[2, k]) * pad_ref[4, k] * th_ref[k]
        o_ref[k] = press_scale * (overlying + 0.5 * weight)
        return overlying + weight

    lax.fori_loop(0, levels, body, jnp.zeros(pad_ref.shape[2:], jnp.float32), unroll=8)


def pressure_run(thickness, padded):
    return pl.pallas_call(
        pressure_kernel,
        out_shape=jax.ShapeDtypeStruct(padded.shape[1:], jnp.float32),
        in_specs=[pl.BlockSpec(memory_space=pltpu.SMEM), pl.BlockSpec(memory_space=pltpu.VMEM)],
        out_specs=pl.BlockSpec(memory_space=pltpu.VMEM),
    )(thickness, padded)


def solve_kernel(th_ref, vel_ref, tra_ref, g0_ref, g1_ref, g2_ref, g3_ref, mix_ref, wet_ref, o_ref, ratio_ref):
    levels = mix_ref.shape[0]
    shape = mix_ref.shape[1:]
    comps = o_ref.shape[0]
    fields = [vel_ref.at[0], vel_ref.at[1], tra_ref.at[0], tra_ref.at[1]]
    grows = [g0_ref, g1_ref, g2_ref, g3_ref]

    def below_of(k):
        nxt = jnp.minimum(k + 1, levels - 1)
        middle = 0.5 * (th_ref[k] + th_ref[nxt])
        coupling = mix_ref[k] * wet_ref[k] * wet_ref[nxt] / middle
        return jnp.where(k < levels - 1, coupling, 0.0)

    def forward(k, carry):
        upper, ratio_prev, value_prev = carry
        below = below_of(k)
        depth = th_ref[k]
        diagonal = depth + upper + below
        divisor = diagonal - upper * ratio_prev
        inverse = 1.0 / divisor
        ratio = below * inverse
        ratio_ref[k] = ratio
        values = []
        for c in range(comps):
            provisional = fields[c][k] * wet_ref[k] + step_main * grows[c][k]
            value = (depth * provisional + upper * value_prev[c]) * inverse
            o_ref[c, k] = value
            values.append(value)
        return (below, ratio, tuple(values))

    zeros = jnp.zeros(shape, jnp.float32)
    lax.fori_loop(0, levels, forward, (zeros, zeros, (zeros,) * comps), unroll=4)

    def backward(step, following):
        k = levels - 1 - step
        ratio = ratio_ref[k]
        results = []
        for c in range(comps):
            result = o_ref[c, k] + ratio * following[c]
            o_ref[c, k] = result
            results.append(result)
        return tuple(results)

    lax.fori_loop(0, levels, backward, (zeros,) * comps, unroll=4)


def solve_columns(velocity, tracers, growth, mixing, wet_mask, thickness):
    return pl.pallas_call(
        solve_kernel,
        out_shape=jax.ShapeDtypeStruct((4,) + mixing.shape, jnp.float32),
        in_specs=[pl.BlockSpec(memory_space=pltpu.SMEM)]
        + [pl.BlockSpec(memory_space=pltpu.VMEM)] * 8,
        out_specs=pl.BlockSpec(memory_space=pltpu.VMEM),
        scratch_shapes=[pltpu.VMEM(mixing.shape, jnp.float32)],
    )(thickness, velocity, tracers, growth[0], growth[1], growth[2], growth[3], mixing, wet_mask)


def solution(mesh):
    return jax.shard_map(
        shards,
        mesh=mesh,
        in_specs=(
            P(None, None, ("gy", "ga"), "gx"),
            P(None, None, ("gy", "ga"), "gx"),
            P(None, ("gy", "ga"), "gx"),
            P(),
            P(("gy", "ga")),
            P(("gy", "ga"), "gx"),
            P(("gy", "ga"), "gx"),
            P(("gy", "ga"), "gx"),
            P(None, ("gy", "ga"), "gx"),
        ),
        out_specs=(
            P(None, None, ("gy", "ga"), "gx"),
            P(None, None, ("gy", "ga"), "gx"),
            P(("gy", "ga"), "gx"),
            P(None, ("gy", "ga"), "gx"),
        ),
        check_vma=False,
    )
```
